128 devices in a mesh: ctx: 8 (over y, core), req: 16 (over x, z).
Axes of the slice: x: 4, y: 4, z: 4, core: 2. Of those that a mesh axis runs over, the one named last changes fastest.
Arguments:
- queries: bfloat16 [16, 512, 1024], P('req', 'ctx'), may hold values from -6 to 6
- keys: bfloat16 [16, 512, 1024], P('req', 'ctx'), may hold values from -6 to 6
- values: bfloat16 [16, 512, 2048], P('req', 'ctx'), may hold values from -6 to 6
- gate_input: bfloat16 [16, 512, 2048], P('req', 'ctx'), may hold values from -6 to 6
- beta: float32 [16, 16, 512], P('req', None, 'ctx'), may hold values from 0.05 to 1
- log_decay: float32 [16, 16, 512], P('req', None, 'ctx'), may hold values from -1 to 0
- norm_gain: float32 [128], replicated, may hold values from 0.1 to 1.9
- w_out: bfloat16 [2048, 2048], replicated, may hold values from -0.125 to 0.125
- hidden: bfloat16 [16, 512, 2048], P('req', 'ctx'), may hold values from -6 to 6
- post_gain: float32 [2048], replicated, may hold values from 0.1 to 1.9
- routes: int32 [16, 512, 10], P('req', 'ctx'), may hold values from 0 to 255, all different within a row; in each aligned block of 64 rows (0 to 63, 64 to 127, ..., all dimensions but the last counted through in order) at most 3 rows name the same one
- route_scores: float32 [16, 512, 10], P('req', 'ctx'), may hold values from 0.1 to 1
- expert_gate_up: bfloat16 [256, 2048, 1024], P(('ctx', 'req')), may hold values from -0.125 to 0.125
- expert_down: bfloat16 [256, 512, 2048], P(('ctx', 'req')), may hold values from -0.25 to 0.25
- accepted: int32 [16], P('req'), may hold values from 1 to 512
Outputs:
- layer_out: bfloat16 [16, 512, 2048], P('req', 'ctx')
- final_state: float32 [16, 16, 128, 128], P('req', 'ctx')
The draws below stay inside these ranges and needn't reach their ends.
Inputs may be any that keep to these rules, and one draw needn't show every extreme that they name: A position's routes name different experts. Among the 64 positions of one device, no expert is named by more than 3 routes, a bound that some block reaches.
All inputs are finite; a program needn't handle non-finite values.
Results may differ from the reference program's by a relative error of at most 0.008.
Values may be sent and summed in bfloat16 or wider, within the bound.
No kernel may reach another device: no remote copies, remote signals or barrier semaphores. Data moves between devices by JAX's collectives and lax.ppermute only.
A program may use at most 128 MiB of HBM per device.

```python
import math
import jax
import jax.numpy as jnp
import numpy as np
from jax import lax

D = 2048
HK = 8
HV = 16
DK = 128
DV = 128
FFE = 512
TOPK = 10
SEQ_DEV = 64
REQS = 16
L = 512
EXPERTS = 256
CAP = 3
DEVICES = 128


def draw_log_decay(key, part):
    keys = jax.random.split(key, 6)
    share = 0.4
    fast = jax.random.uniform(keys[0], (REQS, HV, 1)) < share
    quick_decay_rate = jnp.exp(jax.random.uniform(keys[1], (REQS, HV, 1), minval=math.log(1.0 / 50.0), maxval=math.log(1.0 / 30.0)))
    lagging_factor = jnp.exp(jax.random.uniform(keys[2], (REQS, HV, 1), minval=math.log(0.05 / L), maxval=math.log(0.35 / L)))
    base = jnp.where(fast, quick_decay_rate, lagging_factor)
    block_factor = jnp.exp(jax.random.uniform(keys[3], (REQS, HV, L // SEQ_DEV), minval=math.log(0.5), maxval=math.log(2.0)))
    per_block = jnp.repeat(block_factor, SEQ_DEV, axis=2)
    rough = jax.random.uniform(keys[4], (REQS, HV, L), minval=0.5, maxval=1.5)
    shrink_factor = base * per_block * rough
    cursor_ordinals = jax.random.randint(keys[5], (REQS, 1, 1, 2), 0, L)
    target_ordinals = jnp.arange(L)[None, None, :, None]
    token_bundles = jnp.any(target_ordinals == cursor_ordinals, axis=-1)
    fitting_penalty = jax.random.uniform(jax.random.fold_in(key, 7), (REQS, HV, L), minval=math.log(0.5), maxval=math.log(0.8))
    return jnp.where(token_bundles, fitting_penalty - shrink_factor, -shrink_factor).astype(jnp.float32)


def plant(values, stream_key, smallest, high):
    spot = [jax.random.randint(jax.random.fold_in(stream_key, axis), (), 0, length) for axis, length in enumerate(values.shape)]
    widest = values.shape.index(max(values.shape))
    neighbour = spot[:widest] + [(spot[widest] + 1) % values.shape[widest]] + spot[widest + 1:]
    return values.at[tuple(spot)].set(smallest).at[tuple(neighbour)].set(high)


def level_of(own_key, dims, shards, low, top_value):
    loudness = 1.0
    for dim, shards_of in shards:
        heights = jax.random.uniform(jax.random.fold_in(jax.random.fold_in(own_key, 6), dim), (shards_of,), jnp.float32, low / len(shards), top_value / len(shards))
        loudness = loudness * jnp.repeat(jnp.exp(heights), dims[dim] // shards_of).reshape((-1,) + (1,) * (len(dims) - 1 - dim))
    return loudness


def shared_out(key, own, number, rows, number_of, top, most, skew):
    ranking = jax.random.permutation(key, number_of)
    crowded, usual = load_shares(number_of, rows * top, most, skew, True), load_shares(number_of, rows * top, most, skew, False)
    places = jnp.arange(number_of)

    def named(sizes, offset_by):
        used = int((sizes > 0).sum())
        fixed = max(1, used // 4)
        moved = fixed + (places - fixed + offset_by * (used - fixed)) % max(1, number_of - fixed)
        return jnp.zeros((number_of,), jnp.int32).at[ranking[jnp.where(places < fixed, places, moved)]].set(jnp.asarray(sizes, jnp.int32))

    sizes = jnp.where(number % 4 == 0, named(crowded, number // 4), named(usual, number - number // 4 - 1))
    mixed = jax.random.permutation(jax.random.fold_in(own, 3), number_of)
    source_of, sink = mixed[0:number_of // 2 * 2:2], mixed[1:number_of // 2 * 2:2]
    slack = jnp.minimum(sizes[source_of] - 1, most - sizes[sink]) // 2
    slack = jnp.where((source_of == ranking[0]) | (sink == ranking[0]) | (sizes[sink] == 0), 0, jnp.maximum(slack, 0))
    moved = jax.random.randint(jax.random.fold_in(own, 4), (number_of // 2,), 0, 1 << 20) % (slack + 1)
    sizes = sizes.at[source_of].add(-moved).at[sink].add(moved)
    labels = jnp.searchsorted(jnp.cumsum(sizes), jnp.arange(rows * top), side="right").astype(jnp.int32)
    table = labels.reshape(top, rows).T
    table = table[jax.random.permutation(jax.random.fold_in(own, 1), rows)]
    offset_by = jax.random.randint(jax.random.fold_in(own, 2), (rows, 1), 0, top)
    return jnp.take_along_axis(table, (jnp.arange(top)[None, :] + offset_by) % top, axis=1)


def load_shares(amount, total, bound, lean, full):
    loads = [(1 << 20) // math.isqrt(rank ** lean) + 1 for rank in range(1, amount + 1)]
    largest = bound if full else min(bound, max(-(-total // amount), total * loads[0] // sum(loads)))
    least = 1 if total - largest >= amount - 1 else 0
    holding, spare = [largest] + [least] * (amount - 1), total - largest - least * (amount - 1)
    while spare > 0:
        candidates = [i for i in range(1, amount) if holding[i] < largest] or [i for i in range(1, amount) if holding[i] < bound]
        mass, remaining = sum([loads[i] for i in candidates]), spare
        for i in candidates:
            addition = min(bound - holding[i], max(1, remaining * loads[i] // mass), spare)
            holding[i] = holding[i] + addition
            spare = spare - addition
    return np.array(holding)


def normal_values(key, shape, spread, most, pieces=(), kind=jnp.bfloat16):
    loudness = level_of(key, shape, pieces, -0.22, 0.18) if pieces else 1.0
    entries = jax.random.normal(key, shape, jnp.float32) * spread * loudness
    return jnp.minimum(jnp.maximum(entries, -most), most).astype(kind)


def setup_inputs(seed: int = 0) -> dict:
    arg_keys = jax.random.split(jax.random.key(seed), 16)
    queries = normal_values(arg_keys[0], (REQS, L, HK * DK), 1.0, 6.0, ((0, 16), (1, 8)))
    keys = normal_values(arg_keys[1], (REQS, L, HK * DK), 1.0, 6.0, ((0, 16), (1, 8)))
    values = normal_values(arg_keys[2], (REQS, L, HV * DV), 1.0, 6.0, ((0, 16), (1, 8)))
    gate_input = normal_values(arg_keys[3], (REQS, L, HV * DV), 1.0, 6.0, ((0, 16), (1, 8)))
    beta = jnp.clip(0.05 + 0.95 * jax.random.uniform(arg_keys[4], (REQS, HV, L), jnp.float32) ** level_of(arg_keys[4], (REQS, HV, L), ((0, 16), (2, 8)), -0.2, 0.2), 0.05, 1.0)
    log_decay = draw_log_decay(jax.random.fold_in(arg_keys[15], 71), 0)
    norm_gain = jnp.clip(1.0 + 0.18 * jax.random.normal(arg_keys[6], (DV,), jnp.float32), 0.1, 1.9)
    w_out = normal_values(arg_keys[7], (HV * DV, D), (HV * DV) ** -0.5, 0.125)
    hidden = normal_values(arg_keys[8], (REQS, L, D), 1.0, 6.0, ((0, 16), (1, 8)))
    post_gain = jnp.clip(1.0 + 0.18 * jax.random.normal(arg_keys[9], (D,), jnp.float32), 0.1, 1.9)
    routes_keys = jax.random.split(jax.random.fold_in(arg_keys[10], 1), REQS * L // SEQ_DEV)
    routes_turns = jax.random.permutation(jax.random.fold_in(arg_keys[10], 3), REQS * L // SEQ_DEV)
    routes = jax.vmap(lambda own, number: shared_out(jax.random.fold_in(arg_keys[10], 2), own, number, SEQ_DEV, EXPERTS, TOPK, CAP, 2))(routes_keys, routes_turns).reshape((REQS, L, TOPK))
    route_scores = jnp.clip(jnp.exp(math.log(1.0) - 2.3025851 * jax.random.uniform(arg_keys[11], (REQS, L, TOPK), jnp.float32) ** level_of(arg_keys[11], (REQS, L, TOPK), ((0, 16), (1, 8)), -0.2, 0.2)), 0.1, 1.0)
    expert_gate_up = normal_values(arg_keys[12], (EXPERTS, D, 2 * FFE), D ** -0.5, 0.125, ((0, 128),))
    expert_down = normal_values(arg_keys[13], (EXPERTS, FFE, D), FFE ** -0.5, 0.25, ((0, 128),))
    accepted = plant(jax.random.randint(arg_keys[14], (REQS,), 1, L + 1), jax.random.fold_in(arg_keys[14], 1), 1, L).astype(jnp.int32)
    return dict(queries=queries, keys=keys, values=values, gate_input=gate_input, beta=beta, log_decay=log_decay, norm_gain=norm_gain, w_out=w_out, hidden=hidden, post_gain=post_gain, routes=routes, route_scores=route_scores, expert_gate_up=expert_gate_up, expert_down=expert_down, accepted=accepted)


def unit_rows(x, heads, width):
    x = x.reshape(REQS, L, heads, width).astype(jnp.float32)
    return x * lax.rsqrt(lax.optimization_barrier(jnp.sum(x * x, axis=-1, keepdims=True)) + 1e-06)

def reference(queries, keys, values, gate_input, beta, log_decay, norm_gain, w_out, hidden, post_gain, routes, route_scores, expert_gate_up, expert_down, accepted):
    highest = lax.Precision.HIGHEST
    group = HV // HK
    qh = jnp.repeat(unit_rows(queries, HK, DK), group, axis=2) * DK ** (-0.5)
    kh = jnp.repeat(unit_rows(keys, HK, DK), group, axis=2)
    vh = values.astype(jnp.float32).reshape(REQS, L, HV, DV)
    rates = beta.transpose(0, 2, 1)
    fading = jnp.exp(log_decay).transpose(0, 2, 1)

    def one_request(packed):
        qr, kr, vr, br, gr, length = packed

        def step_forward(carry, inputs):
            state, kept = carry
            q_t, k_t, v_t, b_t, g_t, where_t = inputs
            faded = state * g_t[:, None, None]
            guess = jnp.einsum('hde,hd->he', faded, k_t, precision=highest)
            state = faded + (b_t[:, None] * k_t)[:, :, None] * (v_t - guess)[:, None, :]
            output = jnp.einsum('hde,hd->he', state, q_t, precision=highest)
            kept = jnp.where(where_t == length - 1, state, kept)
            return ((state, kept), output)
        empty = jnp.zeros((HV, DK, DV), jnp.float32)
        target_ordinals = jnp.arange(L, dtype=jnp.int32)
        (last, kept), outputs = lax.scan(step_forward, (empty, empty), (qr, kr, vr, br, gr, target_ordinals))
        return (outputs, kept)
    core, final_state = lax.map(one_request, (qh, kh, vh, rates, fading, accepted))
    scale = lax.rsqrt(lax.optimization_barrier(jnp.mean(core * core, axis=-1, keepdims=True)) + 1e-06)
    gating = jax.nn.silu(gate_input.astype(jnp.float32).reshape(REQS, L, HV, DV))
    normed = (core * scale * norm_gain * gating).reshape(REQS * L, HV * DV).astype(jnp.bfloat16)
    resid = hidden.reshape(REQS * L, D).astype(jnp.float32) + jnp.dot(normed, w_out, preferred_element_type=jnp.float32)
    moe_in = (resid * lax.rsqrt(lax.optimization_barrier(jnp.mean(resid * resid, axis=-1, keepdims=True)) + 1e-06) * post_gain).astype(jnp.bfloat16)
    tokens = REQS * L
    flat_ids = routes.reshape(-1)
    weights = (route_scores / lax.optimization_barrier(jnp.sum(route_scores, axis=-1, keepdims=True))).reshape(-1)
    limit = DEVICES * CAP

    def per_expert(total, expert):
        found = jnp.nonzero(flat_ids == expert, size=limit, fill_value=tokens * TOPK)[0].astype(jnp.int32)
        valid = found < tokens * TOPK
        safe = jnp.where(valid, found, 0).astype(jnp.int32)
        owners = (safe // TOPK).astype(jnp.int32)
        rows = moe_in[owners]
        both = jnp.dot(rows, expert_gate_up[expert], preferred_element_type=jnp.float32)
        inner = (jax.nn.silu(both[:, :FFE]) * both[:, FFE:]).astype(jnp.bfloat16)
        result = jnp.dot(inner, expert_down[expert], preferred_element_type=jnp.float32).astype(jnp.bfloat16)
        result = lax.optimization_barrier(result).astype(jnp.float32)
        term = result * jnp.where(valid, weights[safe], 0.0)[:, None]
        return (total.at[owners].add(term), None)
    moe_out, unused = lax.scan(per_expert, jnp.zeros((tokens, D), jnp.float32), jnp.arange(EXPERTS, dtype=jnp.int32))
    layer_out = (resid + moe_out).astype(jnp.bfloat16).reshape(REQS, L, D)
    return (layer_out, final_state)
```

```python
import jax
import jax.numpy as jnp
from jax import lax
from jax.sharding import PartitionSpec as P

D = 2048
HK = 8
HV = 16
DK = 128
DV = 128
FFE = 512
TOPK = 10
EXP_DEV = 2


def unit_rows(x):
    x = x.astype(jnp.float32)
    return x * lax.rsqrt(jnp.sum(x * x, axis=-1, keepdims=True) + 1e-06)


def unit_lower_inverse(lower):
    highest = lax.Precision.HIGHEST
    n = lower.shape[-1]
    rows = jnp.arange(n)[:, None]
    cols = jnp.arange(n)[None, :]
    inv = None
    b = 1
    while b < n:
        sel = (rows // (2 * b) == cols // (2 * b)) & ((rows // b) % 2 == 1) & ((cols // b) % 2 == 0)
        c = jnp.where(sel, lower, 0.0)
        if inv is None:
            inv = lax.optimization_barrier(jnp.eye(n, dtype=lower.dtype) - c)
        else:
            mc = jnp.einsum("...ij,...jk->...ik", inv, c, precision=highest)
            inv = inv - jnp.einsum("...ij,...jk->...ik", mc, inv, precision=highest)
        b *= 2
    return inv


def run_experts(arrived, expert_gate_up, expert_down):
    provider_rows, count, part, width = arrived.shape
    rows = arrived.transpose(1, 0, 2, 3).reshape(count, provider_rows * part, width)
    both = jnp.einsum("erd,edf->erf", rows, expert_gate_up, preferred_element_type=jnp.float32)
    inner = (jax.nn.silu(both[..., :FFE]) * both[..., FFE:]).astype(jnp.bfloat16)
    result = jnp.einsum(
        "erf,efd->erd", inner, expert_down, preferred_element_type=jnp.float32
    ).astype(jnp.bfloat16)
    return result.reshape(count, provider_rows, part, width).transpose(1, 0, 2, 3)


def shards(
    queries,
    keys,
    values,
    gate_input,
    beta,
    log_decay,
    norm_gain,
    w_out,
    hidden,
    post_gain,
    routes,
    route_scores,
    expert_gate_up,
    expert_down,
    accepted,
):
    highest = lax.Precision.HIGHEST
    seq = queries.shape[1]
    n_ctx = lax.axis_size("ctx")
    n_req = lax.axis_size("req")
    n_dev = n_ctx * n_req
    experts = EXP_DEV * n_dev
    cap = max(2, 3 * seq * TOPK // (2 * experts))
    kh_dev = HK // n_ctx
    hv_dev = HV // n_ctx
    qw = kh_dev * DK
    vw = hv_dev * DV

    packed = jnp.concatenate(
        [
            queries[0].reshape(seq, n_ctx, qw),
            keys[0].reshape(seq, n_ctx, qw),
            values[0].reshape(seq, n_ctx, vw),
            gate_input[0].reshape(seq, n_ctx, vw),
        ],
        axis=2,
    ).transpose(1, 0, 2)
    arrived = lax.all_to_all(packed, "ctx", 0, 0, tiled=True)
    rates_decay = (
        jnp.stack([beta[0], log_decay[0]]).reshape(2, n_ctx, hv_dev, seq).transpose(1, 0, 2, 3)
    )
    rd = lax.all_to_all(rates_decay, "ctx", 0, 0, tiled=True)
    rates = rd[:, 0].transpose(1, 0, 2)
    gamma = jnp.cumsum(rd[:, 1].transpose(1, 0, 2), axis=-1)
    qc = unit_rows(arrived[..., :qw]) * DK ** (-0.5)
    kc = unit_rows(arrived[..., qw : 2 * qw])
    vc = (
        arrived[..., 2 * qw : 2 * qw + vw]
        .astype(jnp.float32)
        .reshape(n_ctx, seq, hv_dev, DV)
        .transpose(2, 0, 1, 3)
    )
    gc = arrived[..., 2 * qw + vw :].reshape(n_ctx, seq, hv_dev, DV)

    ordinals = jnp.arange(seq)
    before = ordinals[:, None] > ordinals[None, :]
    upto = ordinals[:, None] >= ordinals[None, :]
    spans = gamma[..., :, None] - gamma[..., None, :]
    pair_decay = jnp.exp(jnp.where(upto, spans, 0.0))
    key_key = jnp.einsum("ntd,nsd->nts", kc, kc, precision=highest)
    lower = jnp.where(before, pair_decay * key_key[None] * rates[..., None, :], 0.0)
    inverse = unit_lower_inverse(lower)
    growth = jnp.exp(gamma)
    right = jnp.concatenate(
        [vc, growth[..., None] * jnp.broadcast_to(kc[None], vc.shape)], axis=-1
    )
    solved = jnp.einsum("hnts,hnsf->hntf", inverse, right, precision=highest)
    solved_values = solved[..., :DV]
    solved_keys = solved[..., DV:]
    tail = rates * jnp.exp(gamma[..., -1:] - gamma)
    weighted = kc[None] * tail[..., None]
    identity = jnp.eye(DK, dtype=jnp.float32)
    transfer = growth[..., -1, None, None] * identity - jnp.einsum(
        "hntd,hnte->hnde", weighted, solved_keys, precision=highest
    )
    offset = jnp.einsum("hntd,hnte->hnde", weighted, solved_values, precision=highest)
    state = jnp.zeros((hv_dev, DK, DV), jnp.float32)
    states = [state]
    for n in range(n_ctx - 1):
        state = offset[:, n] + jnp.einsum(
            "hde,hef->hdf", transfer[:, n], state, precision=highest
        )
        states.append(state)
    states = jnp.stack(states, axis=1)
    pseudo = solved_values - jnp.einsum("hntd,hnde->hnte", solved_keys, states, precision=highest)
    query_key = jnp.einsum("ntd,nsd->nts", qc, kc, precision=highest)
    mixing = jnp.where(upto, pair_decay * query_key[None] * rates[..., None, :], 0.0)
    core = growth[..., None] * jnp.einsum("ntd,hnde->hnte", qc, states, precision=highest)
    core = core + jnp.einsum("hnts,hnse->hnte", mixing, pseudo, precision=highest)

    last = accepted[0] - 1
    chunk = last // seq
    local = last % seq
    gamma_chunk = lax.dynamic_index_in_dim(gamma, chunk, axis=1, keepdims=False)
    rates_chunk = lax.dynamic_index_in_dim(rates, chunk, axis=1, keepdims=False)
    pseudo_chunk = lax.dynamic_index_in_dim(pseudo, chunk, axis=1, keepdims=False)
    state_chunk = lax.dynamic_index_in_dim(states, chunk, axis=1, keepdims=False)
    keys_chunk = lax.dynamic_index_in_dim(kc, chunk, axis=0, keepdims=False)
    gamma_at = lax.dynamic_index_in_dim(gamma_chunk, local, axis=1, keepdims=False)
    keep = jnp.where(
        ordinals[None, :] <= local,
        rates_chunk * jnp.exp(jnp.minimum(gamma_at[:, None] - gamma_chunk, 0.0)),
        0.0,
    )
    final_state = jnp.exp(gamma_at)[:, None, None] * state_chunk + jnp.einsum(
        "td,hte->hde", keys_chunk, keep[..., None] * pseudo_chunk, precision=highest
    )
    final_state = final_state[None]

    scale = lax.rsqrt(jnp.mean(core * core, axis=-1, keepdims=True) + 1e-06)
    gating = jax.nn.silu(gc.astype(jnp.float32).transpose(2, 0, 1, 3))
    normed = (core * scale * norm_gain * gating).astype(jnp.bfloat16)
    normed = normed.transpose(1, 2, 0, 3).reshape(n_ctx, seq, vw)
    back = lax.all_to_all(normed, "ctx", 0, 0, tiled=True)
    resid = hidden[0].astype(jnp.float32) + jnp.einsum(
        "jtf,jfd->td",
        back,
        w_out.reshape(n_ctx, vw, D),
        preferred_element_type=jnp.float32,
    )
    moe_in = (
        resid * lax.rsqrt(jnp.mean(resid * resid, axis=-1, keepdims=True) + 1e-06) * post_gain
    ).astype(jnp.bfloat16)

    flat_ids = routes[0].reshape(-1)
    onehot = (flat_ids[:, None] == jnp.arange(experts, dtype=jnp.int32)[None, :]).astype(jnp.int32)
    earlier = jnp.cumsum(onehot, axis=0) - onehot
    slot = jnp.sum(earlier * onehot, axis=1)
    target = (flat_ids * cap + slot).reshape(seq, TOPK)
    slots = jnp.arange(experts * cap, dtype=jnp.int32)
    hits = target[None, :, :] == slots[:, None, None]
    dispatch = jnp.sum(jnp.where(hits, 1.0, 0.0), axis=-1).astype(jnp.bfloat16)
    outgoing_rows = jnp.dot(dispatch, moe_in, preferred_element_type=jnp.float32).astype(
        jnp.bfloat16
    )
    returned = lax.all_to_all(
        run_experts(
            lax.all_to_all(
                outgoing_rows.reshape(n_dev, EXP_DEV, cap, D),
                ("ctx", "req"),
                split_axis=0,
                concat_axis=0,
                tiled=True,
            ),
            expert_gate_up,
            expert_down,
        ),
        ("ctx", "req"),
        split_axis=0,
        concat_axis=0,
        tiled=True,
    )
    scores = route_scores[0]
    mix_weights = scores / jnp.sum(scores, axis=-1, keepdims=True)
    combine = jnp.sum(jnp.where(hits, mix_weights[None], 0.0), axis=-1).T
    moe_out = jnp.dot(
        combine,
        returned.reshape(experts * cap, D).astype(jnp.float32),
        precision=highest,
    )
    layer_out = (resid + moe_out).astype(jnp.bfloat16)[None]
    return (layer_out, final_state)


def solution(mesh):
    placed = (
        P("req", "ctx", None),
        P("req", "ctx", None),
        P("req", "ctx", None),
        P("req", "ctx", None),
        P("req", None, "ctx"),
        P("req", None, "ctx"),
        P(),
        P(),
        P("req", "ctx", None),
        P(),
        P("req", "ctx", None),
        P("req", "ctx", None),
        P(("ctx", "req"), None, None),
        P(("ctx", "req"), None, None),
        P("req"),
    )
    return jax.shard_map(
        shards,
        mesh=mesh,
        in_specs=placed,
        out_specs=(P("req", "ctx", None), P("req", "ctx", None, None)),
        check_vma=False,
    )
```

```python
import jax
import jax.numpy as jnp
from jax import lax
from jax.sharding import PartitionSpec as P

D = 2048
HK = 8
HV = 16
DK = 128
DV = 128
FFE = 512
TOPK = 10
EXP_DEV = 2


def unit_rows(x):
    x = x.astype(jnp.float32)
    return x * lax.rsqrt(jnp.sum(x * x, axis=-1, keepdims=True) + 1e-06)


def unit_lower_inverse(lower):
    highest = lax.Precision.HIGHEST
    n = lower.shape[-1]
    rows = jnp.arange(n)[:, None]
    cols = jnp.arange(n)[None, :]
    inv = None
    b = 1
    while b < n:
        sel = (rows // (2 * b) == cols // (2 * b)) & ((rows // b) % 2 == 1) & ((cols // b) % 2 == 0)
        c = jnp.where(sel, lower, 0.0)
        if inv is None:
            inv = lax.optimization_barrier(jnp.eye(n, dtype=lower.dtype) - c)
        else:
            mc = jnp.einsum("...ij,...jk->...ik", inv, c, precision=highest)
            inv = inv - jnp.einsum("...ij,...jk->...ik", mc, inv, precision=highest)
        b *= 2
    return inv


def run_experts(arrived, expert_gate_up, expert_down):
    provider_rows, count, part, width = arrived.shape
    rows = arrived.transpose(1, 0, 2, 3).reshape(count, provider_rows * part, width)
    both = jnp.einsum("erd,edf->erf", rows, expert_gate_up, preferred_element_type=jnp.float32)
    inner = (jax.nn.silu(both[..., :FFE]) * both[..., FFE:]).astype(jnp.bfloat16)
    result = jnp.einsum(
        "erf,efd->erd", inner, expert_down, preferred_element_type=jnp.float32
    ).astype(jnp.bfloat16)
    return result.reshape(count, provider_rows, part, width).transpose(1, 0, 2, 3)


def shards(
    queries,
    keys,
    values,
    gate_input,
    beta,
    log_decay,
    norm_gain,
    w_out,
    hidden,
    post_gain,
    routes,
    route_scores,
    expert_gate_up,
    expert_down,
    accepted,
):
    highest = lax.Precision.HIGHEST
    seq = queries.shape[1]
    n_ctx = lax.axis_size("ctx")
    n_req = lax.axis_size("req")
    n_dev = n_ctx * n_req
    experts = EXP_DEV * n_dev
    cap = max(2, 3 * seq * TOPK // (2 * experts))
    kh_dev = HK // n_ctx
    hv_dev = HV // n_ctx
    qw = kh_dev * DK
    vw = hv_dev * DV

    packed = jnp.concatenate(
        [
            queries[0].reshape(seq, n_ctx, qw),
            keys[0].reshape(seq, n_ctx, qw),
            values[0].reshape(seq, n_ctx, vw),
            gate_input[0].reshape(seq, n_ctx, vw),
        ],
        axis=2,
    ).transpose(1, 0, 2)
    arrived = lax.all_to_all(packed, "ctx", 0, 0, tiled=True)
    rates_decay = (
        jnp.stack([beta[0], log_decay[0]]).reshape(2, n_ctx, hv_dev, seq).transpose(1, 0, 2, 3)
    )
    rd = lax.all_to_all(rates_decay, "ctx", 0, 0, tiled=True)
    rates = rd[:, 0].transpose(1, 0, 2)
    gamma = jnp.cumsum(rd[:, 1].transpose(1, 0, 2), axis=-1)
    qc = unit_rows(arrived[..., :qw]) * DK ** (-0.5)
    kc = unit_rows(arrived[..., qw : 2 * qw])
    vc = (
        arrived[..., 2 * qw : 2 * qw + vw]
        .astype(jnp.float32)
        .reshape(n_ctx, seq, hv_dev, DV)
        .transpose(2, 0, 1, 3)
    )
    gc = arrived[..., 2 * qw + vw :].reshape(n_ctx, seq, hv_dev, DV)

    ordinals = jnp.arange(seq)
    before = ordinals[:, None] > ordinals[None, :]
    upto = ordinals[:, None] >= ordinals[None, :]
    spans = gamma[..., :, None] - gamma[..., None, :]
    pair_decay = jnp.exp(jnp.where(upto, spans, 0.0))
    key_key = jnp.einsum("ntd,nsd->nts", kc, kc, precision=highest)
    lower = jnp.where(before, pair_decay * key_key[None] * rates[..., None, :], 0.0)
    inverse = unit_lower_inverse(lower)
    growth = jnp.exp(gamma)
    right = jnp.concatenate(
        [vc, growth[..., None] * jnp.broadcast_to(kc[None], vc.shape)], axis=-1
    )
    solved = jnp.einsum("hnts,hnsf->hntf", inverse, right, precision=highest)
    solved_values = solved[..., :DV]
    solved_keys = solved[..., DV:]
    tail = rates * jnp.exp(gamma[..., -1:] - gamma)
    weighted = kc[None] * tail[..., None]
    identity = jnp.eye(DK, dtype=jnp.float32)
    transfer = growth[..., -1, None, None] * identity - jnp.einsum(
        "hntd,hnte->hnde", weighted, solved_keys, precision=highest
    )
    offset = jnp.einsum("hntd,hnte->hnde", weighted, solved_values, precision=highest)
    state = jnp.zeros((hv_dev, DK, DV), jnp.float32)
    states = [state]
    for n in range(n_ctx - 1):
        state = offset[:, n] + jnp.einsum(
            "hde,hef->hdf", transfer[:, n], state, precision=highest
        )
        states.append(state)
    states = jnp.stack(states, axis=1)
    pseudo = solved_values - jnp.einsum("hntd,hnde->hnte", solved_keys, states, precision=highest)
    query_key = jnp.einsum("ntd,nsd->nts", qc, kc, precision=highest)
    mixing = jnp.where(upto, pair_decay * query_key[None] * rates[..., None, :], 0.0)
    core = growth[..., None] * jnp.einsum("ntd,hnde->hnte", qc, states, precision=highest)
    core = core + jnp.einsum("hnts,hnse->hnte", mixing, pseudo, precision=highest)

    last = accepted[0] - 1
    chunk = last // seq
    local = last % seq
    gamma_chunk = lax.dynamic_index_in_dim(gamma, chunk, axis=1, keepdims=False)
    rates_chunk = lax.dynamic_index_in_dim(rates, chunk, axis=1, keepdims=False)
    pseudo_chunk = lax.dynamic_index_in_dim(pseudo, chunk, axis=1, keepdims=False)
    state_chunk = lax.dynamic_index_in_dim(states, chunk, axis=1, keepdims=False)
    keys_chunk = lax.dynamic_index_in_dim(kc, chunk, axis=0, keepdims=False)
    gamma_at = lax.dynamic_index_in_dim(gamma_chunk, local, axis=1, keepdims=False)
    keep = jnp.where(
        ordinals[None, :] <= local,
        rates_chunk * jnp.exp(jnp.minimum(gamma_at[:, None] - gamma_chunk, 0.0)),
        0.0,
    )
    final_state = jnp.exp(gamma_at)[:, None, None] * state_chunk + jnp.einsum(
        "td,hte->hde", keys_chunk, keep[..., None] * pseudo_chunk, precision=highest
    )
    final_state = final_state[None]

    scale = lax.rsqrt(jnp.mean(core * core, axis=-1, keepdims=True) + 1e-06)
    gating = jax.nn.silu(gc.astype(jnp.float32).transpose(2, 0, 1, 3))
    normed = (core * scale * norm_gain * gating).astype(jnp.bfloat16)
    normed = normed.transpose(1, 2, 0, 3).reshape(n_ctx, seq, vw)
    back = lax.all_to_all(normed, "ctx", 0, 0, tiled=True)
    resid = hidden[0].astype(jnp.float32) + jnp.einsum(
        "jtf,jfd->td",
        back,
        w_out.reshape(n_ctx, vw, D),
        preferred_element_type=jnp.float32,
    )
    moe_in = (
        resid * lax.rsqrt(jnp.mean(resid * resid, axis=-1, keepdims=True) + 1e-06) * post_gain
    ).astype(jnp.bfloat16)

    flat_ids = routes[0].reshape(-1)
    onehot = (flat_ids[:, None] == jnp.arange(experts, dtype=jnp.int32)[None, :]).astype(jnp.int32)
    earlier = jnp.cumsum(onehot, axis=0) - onehot
    slot = jnp.sum(earlier * onehot, axis=1)
    target = (flat_ids * cap + slot).reshape(seq, TOPK)
    slots = (
        jnp.arange(experts * cap, dtype=jnp.int32)
        .reshape(n_dev, EXP_DEV, cap)
        .transpose(0, 2, 1)
    )
    hits = target[None, None, None, :, :] == slots[..., None, None]
    dispatch = jnp.sum(jnp.where(hits, 1.0, 0.0), axis=-1).astype(jnp.bfloat16)
    outgoing_rows = jnp.einsum(
        "dcet,tf->dcef", dispatch, moe_in, preferred_element_type=jnp.float32
    ).astype(jnp.bfloat16)
    arrived_rows = lax.all_to_all(
        outgoing_rows, ("ctx", "req"), split_axis=0, concat_axis=0, tiled=True
    )
    both = jnp.einsum(
        "scex,exf->escf", arrived_rows, expert_gate_up, preferred_element_type=jnp.float32
    )
    inner = (jax.nn.silu(both[..., :FFE]) * both[..., FFE:]).astype(jnp.bfloat16)
    result = jnp.einsum(
        "escf,efx->scex", inner, expert_down, preferred_element_type=jnp.float32
    ).astype(jnp.bfloat16)
    returned = lax.all_to_all(result, ("ctx", "req"), split_axis=0, concat_axis=0, tiled=True)
    scores = route_scores[0]
    mix_weights = scores / jnp.sum(scores, axis=-1, keepdims=True)
    combine = jnp.sum(jnp.where(hits, mix_weights, 0.0), axis=-1)
    moe_out = jnp.einsum(
        "dcet,dcex->tx",
        combine,
        returned.astype(jnp.float32),
        precision=highest,
    )
    layer_out = (resid + moe_out).astype(jnp.bfloat16)[None]
    return (layer_out, final_state)


def solution(mesh):
    placed = (
        P("req", "ctx", None),
        P("req", "ctx", None),
        P("req", "ctx", None),
        P("req", "ctx", None),
        P("req", None, "ctx"),
        P("req", None, "ctx"),
        P(),
        P(),
        P("req", "ctx", None),
        P(),
        P("req", "ctx", None),
        P("req", "ctx", None),
        P(("ctx", "req"), None, None),
        P(("ctx", "req"), None, None),
        P("req"),
    )
    return jax.shard_map(
        shards,
        mesh=mesh,
        in_specs=placed,
        out_specs=(P("req", "ctx", None), P("req", "ctx", None, None)),
        check_vma=False,
    )
```

```python
import jax
import jax.numpy as jnp
from jax import lax
from jax.sharding import PartitionSpec as P

D = 2048
HK = 8
HV = 16
DK = 128
DV = 128
FFE = 512
TOPK = 10
EXP_DEV = 2


def unit_rows(x):
    x = x.astype(jnp.float32)
    return x * lax.rsqrt(jnp.sum(x * x, axis=-1, keepdims=True) + 1e-06)


def unit_lower_inverse(lower):
    highest = lax.Precision.HIGHEST
    n = lower.shape[-1]
    rows = jnp.arange(n)[:, None]
    cols = jnp.arange(n)[None, :]
    inv = None
    b = 1
    while b < n:
        sel = (rows // (2 * b) == cols // (2 * b)) & ((rows // b) % 2 == 1) & ((cols // b) % 2 == 0)
        c = jnp.where(sel, lower, 0.0)
        if inv is None:
            inv = lax.optimization_barrier(jnp.eye(n, dtype=lower.dtype) - c)
        else:
            mc = jnp.einsum("...ij,...jk->...ik", inv, c, precision=highest)
            inv = inv - jnp.einsum("...ij,...jk->...ik", mc, inv, precision=highest)
        b *= 2
    return inv


def run_experts(arrived, expert_gate_up, expert_down):
    provider_rows, count, part, width = arrived.shape
    rows = arrived.transpose(1, 0, 2, 3).reshape(count, provider_rows * part, width)
    both = jnp.einsum("erd,edf->erf", rows, expert_gate_up, preferred_element_type=jnp.float32)
    inner = (jax.nn.silu(both[..., :FFE]) * both[..., FFE:]).astype(jnp.bfloat16)
    result = jnp.einsum(
        "erf,efd->erd", inner, expert_down, preferred_element_type=jnp.float32
    ).astype(jnp.bfloat16)
    return result.reshape(count, provider_rows, part, width).transpose(1, 0, 2, 3)


def shards(
    queries,
    keys,
    values,
    gate_input,
    beta,
    log_decay,
    norm_gain,
    w_out,
    hidden,
    post_gain,
    routes,
    route_scores,
    expert_gate_up,
    expert_down,
    accepted,
):
    highest = lax.Precision.HIGHEST
    seq = queries.shape[1]
    n_ctx = lax.axis_size("ctx")
    n_req = lax.axis_size("req")
    n_dev = n_ctx * n_req
    experts = EXP_DEV * n_dev
    cap = max(2, 3 * seq * TOPK // (2 * experts))
    kh_dev = HK // n_ctx
    hv_dev = HV // n_ctx
    qw = kh_dev * DK
    vw = hv_dev * DV

    rates_decay = (
        jnp.stack([beta[0], log_decay[0]]).reshape(2, n_ctx, hv_dev, seq).transpose(1, 0, 2, 3)
    )
    hi = lax.reduce_precision(rates_decay, exponent_bits=8, mantissa_bits=7)
    rest = rates_decay - hi
    mid = lax.reduce_precision(rest, exponent_bits=8, mantissa_bits=7)
    lo = lax.reduce_precision(rest - mid, exponent_bits=8, mantissa_bits=7)
    parts = jnp.stack([hi, mid, lo], axis=1).astype(jnp.bfloat16).reshape(n_ctx, 1, -1)
    width = 2 * qw + 2 * vw
    packed = jnp.concatenate(
        [
            jnp.concatenate(
                [
                    queries[0].reshape(seq, n_ctx, qw),
                    keys[0].reshape(seq, n_ctx, qw),
                    values[0].reshape(seq, n_ctx, vw),
                    gate_input[0].reshape(seq, n_ctx, vw),
                ],
                axis=2,
            ).transpose(1, 0, 2),
            jnp.pad(parts, ((0, 0), (0, 0), (0, width - parts.shape[-1]))),
        ],
        axis=1,
    )
    got = lax.all_to_all(packed, "ctx", 0, 0, tiled=True)
    arrived = got[:, :seq]
    rd = (
        got[:, seq, : parts.shape[-1]]
        .astype(jnp.float32)
        .reshape(n_ctx, 3, 2, hv_dev, seq)
    )
    rd = (rd[:, 0] + rd[:, 1]) + rd[:, 2]
    rates = rd[:, 0].transpose(1, 0, 2)
    gamma = jnp.cumsum(rd[:, 1].transpose(1, 0, 2), axis=-1)
    qc = unit_rows(arrived[..., :qw]) * DK ** (-0.5)
    kc = unit_rows(arrived[..., qw : 2 * qw])
    vc = (
        arrived[..., 2 * qw : 2 * qw + vw]
        .astype(jnp.float32)
        .reshape(n_ctx, seq, hv_dev, DV)
        .transpose(2, 0, 1, 3)
    )
    gc = arrived[..., 2 * qw + vw :].reshape(n_ctx, seq, hv_dev, DV)

    ordinals = jnp.arange(seq)
    before = ordinals[:, None] > ordinals[None, :]
    upto = ordinals[:, None] >= ordinals[None, :]
    spans = gamma[..., :, None] - gamma[..., None, :]
    pair_decay = jnp.exp(jnp.where(upto, spans, 0.0))
    key_key = jnp.einsum("ntd,nsd->nts", kc, kc, precision=highest)
    lower = jnp.where(before, pair_decay * key_key[None] * rates[..., None, :], 0.0)
    inverse = unit_lower_inverse(lower)
    growth = jnp.exp(gamma)
    right = jnp.concatenate(
        [vc, growth[..., None] * jnp.broadcast_to(kc[None], vc.shape)], axis=-1
    )
    solved = jnp.einsum("hnts,hnsf->hntf", inverse, right, precision=highest)
    solved_values = solved[..., :DV]
    solved_keys = solved[..., DV:]
    tail = rates * jnp.exp(gamma[..., -1:] - gamma)
    weighted = kc[None] * tail[..., None]
    identity = jnp.eye(DK, dtype=jnp.float32)
    transfer = growth[..., -1, None, None] * identity - jnp.einsum(
        "hntd,hnte->hnde", weighted, solved_keys, precision=highest
    )
    offset = jnp.einsum("hntd,hnte->hnde", weighted, solved_values, precision=highest)
    state = jnp.zeros((hv_dev, DK, DV), jnp.float32)
    states = [state]
    for n in range(n_ctx - 1):
        state = offset[:, n] + jnp.einsum(
            "hde,hef->hdf", transfer[:, n], state, precision=highest
        )
        states.append(state)
    states = jnp.stack(states, axis=1)
    pseudo = solved_values - jnp.einsum("hntd,hnde->hnte", solved_keys, states, precision=highest)
    query_key = jnp.einsum("ntd,nsd->nts", qc, kc, precision=highest)
    mixing = jnp.where(upto, pair_decay * query_key[None] * rates[..., None, :], 0.0)
    core = growth[..., None] * jnp.einsum("ntd,hnde->hnte", qc, states, precision=highest)
    core = core + jnp.einsum("hnts,hnse->hnte", mixing, pseudo, precision=highest)

    last = accepted[0] - 1
    chunk = last // seq
    local = last % seq
    gamma_chunk = lax.dynamic_index_in_dim(gamma, chunk, axis=1, keepdims=False)
    rates_chunk = lax.dynamic_index_in_dim(rates, chunk, axis=1, keepdims=False)
    pseudo_chunk = lax.dynamic_index_in_dim(pseudo, chunk, axis=1, keepdims=False)
    state_chunk = lax.dynamic_index_in_dim(states, chunk, axis=1, keepdims=False)
    keys_chunk = lax.dynamic_index_in_dim(kc, chunk, axis=0, keepdims=False)
    gamma_at = lax.dynamic_index_in_dim(gamma_chunk, local, axis=1, keepdims=False)
    keep = jnp.where(
        ordinals[None, :] <= local,
        rates_chunk * jnp.exp(jnp.minimum(gamma_at[:, None] - gamma_chunk, 0.0)),
        0.0,
    )
    final_state = jnp.exp(gamma_at)[:, None, None] * state_chunk + jnp.einsum(
        "td,hte->hde", keys_chunk, keep[..., None] * pseudo_chunk, precision=highest
    )
    final_state = final_state[None]

    scale = lax.rsqrt(jnp.mean(core * core, axis=-1, keepdims=True) + 1e-06)
    gating = jax.nn.silu(gc.astype(jnp.float32).transpose(2, 0, 1, 3))
    normed = (core * scale * norm_gain * gating).astype(jnp.bfloat16)
    normed = normed.transpose(1, 2, 0, 3).reshape(n_ctx, seq, vw)
    back = lax.all_to_all(normed, "ctx", 0, 0, tiled=True)
    resid = hidden[0].astype(jnp.float32) + jnp.einsum(
        "jtf,jfd->td",
        back,
        w_out.reshape(n_ctx, vw, D),
        preferred_element_type=jnp.float32,
    )
    moe_in = (
        resid * lax.rsqrt(jnp.mean(resid * resid, axis=-1, keepdims=True) + 1e-06) * post_gain
    ).astype(jnp.bfloat16)

    flat_ids = routes[0].reshape(-1)
    onehot = (flat_ids[:, None] == jnp.arange(experts, dtype=jnp.int32)[None, :]).astype(jnp.int32)
    earlier = jnp.cumsum(onehot, axis=0) - onehot
    slot = jnp.sum(earlier * onehot, axis=1)
    target = (flat_ids * cap + slot).reshape(seq, TOPK)
    slots = (
        jnp.arange(experts * cap, dtype=jnp.int32)
        .reshape(n_dev, EXP_DEV, cap)
        .transpose(0, 2, 1)
    )
    hits = target[None, None, None, :, :] == slots[..., None, None]
    dispatch = jnp.sum(jnp.where(hits, 1.0, 0.0), axis=-1).astype(jnp.bfloat16)
    outgoing_rows = jnp.einsum(
        "dcet,tf->dcef", dispatch, moe_in, preferred_element_type=jnp.float32
    ).astype(jnp.bfloat16)
    arrived_rows = lax.all_to_all(
        outgoing_rows, ("ctx", "req"), split_axis=0, concat_axis=0, tiled=True
    )
    both = jnp.einsum(
        "scex,exf->escf", arrived_rows, expert_gate_up, preferred_element_type=jnp.float32
    )
    inner = (jax.nn.silu(both[..., :FFE]) * both[..., FFE:]).astype(jnp.bfloat16)
    result = jnp.einsum(
        "escf,efx->scex", inner, expert_down, preferred_element_type=jnp.float32
    ).astype(jnp.bfloat16)
    returned = lax.all_to_all(result, ("ctx", "req"), split_axis=0, concat_axis=0, tiled=True)
    scores = route_scores[0]
    mix_weights = scores / jnp.sum(scores, axis=-1, keepdims=True)
    combine = jnp.sum(jnp.where(hits, mix_weights, 0.0), axis=-1)
    combine_hi = lax.reduce_precision(combine, exponent_bits=8, mantissa_bits=7)
    combine_lo = combine - combine_hi
    halves = jnp.concatenate([combine_hi, combine_lo], axis=-1).astype(jnp.bfloat16)
    both_out = jnp.einsum(
        "dcet,dcex->tx", halves, returned, preferred_element_type=jnp.float32
    )
    moe_out = both_out[:seq] + both_out[seq:]
    layer_out = (resid + moe_out).astype(jnp.bfloat16)[None]
    return (layer_out, final_state)


def solution(mesh):
    placed = (
        P("req", "ctx", None),
        P("req", "ctx", None),
        P("req", "ctx", None),
        P("req", "ctx", None),
        P("req", None, "ctx"),
        P("req", None, "ctx"),
        P(),
        P(),
        P("req", "ctx", None),
        P(),
        P("req", "ctx", None),
        P("req", "ctx", None),
        P(("ctx", "req"), None, None),
        P(("ctx", "req"), None, None),
        P("req"),
    )
    return jax.shard_map(
        shards,
        mesh=mesh,
        in_specs=placed,
        out_specs=(P("req", "ctx", None), P("req", "ctx", None, None)),
        check_vma=False,
    )
```

```python
import jax
import jax.numpy as jnp
from jax import lax
from jax.sharding import PartitionSpec as P

D = 2048
HK = 8
HV = 16
DK = 128
DV = 128
FFE = 512
TOPK = 10
EXP_DEV = 2


def unit_rows(x):
    x = x.astype(jnp.float32)
    return x * lax.rsqrt(jnp.sum(x * x, axis=-1, keepdims=True) + 1e-06)


def unit_lower_inverse(lower):
    highest = lax.Precision.HIGHEST
    n = lower.shape[-1]
    rows = jnp.arange(n)[:, None]
    cols = jnp.arange(n)[None, :]
    inv = None
    b = 1
    while b < n:
        sel = (rows // (2 * b) == cols // (2 * b)) & ((rows // b) % 2 == 1) & ((cols // b) % 2 == 0)
        c = jnp.where(sel, lower, 0.0)
        if inv is None:
            inv = lax.optimization_barrier(jnp.eye(n, dtype=lower.dtype) - c)
        else:
            mc = jnp.einsum("...ij,...jk->...ik", inv, c, precision=highest)
            inv = inv - jnp.einsum("...ij,...jk->...ik", mc, inv, precision=highest)
        b *= 2
    return inv


def run_experts(arrived, expert_gate_up, expert_down):
    provider_rows, count, part, width = arrived.shape
    rows = arrived.transpose(1, 0, 2, 3).reshape(count, provider_rows * part, width)
    both = jnp.einsum("erd,edf->erf", rows, expert_gate_up, preferred_element_type=jnp.float32)
    inner = (jax.nn.silu(both[..., :FFE]) * both[..., FFE:]).astype(jnp.bfloat16)
    result = jnp.einsum(
        "erf,efd->erd", inner, expert_down, preferred_element_type=jnp.float32
    ).astype(jnp.bfloat16)
    return result.reshape(count, provider_rows, part, width).transpose(1, 0, 2, 3)


def shards(
    queries,
    keys,
    values,
    gate_input,
    beta,
    log_decay,
    norm_gain,
    w_out,
    hidden,
    post_gain,
    routes,
    route_scores,
    expert_gate_up,
    expert_down,
    accepted,
):
    highest = lax.Precision.HIGHEST
    seq = queries.shape[1]
    n_ctx = lax.axis_size("ctx")
    n_req = lax.axis_size("req")
    n_dev = n_ctx * n_req
    experts = EXP_DEV * n_dev
    cap = max(2, 3 * seq * TOPK // (2 * experts))
    kh_dev = HK // n_ctx
    hv_dev = HV // n_ctx
    qw = kh_dev * DK
    vw = hv_dev * DV

    rates_decay = (
        jnp.stack([beta[0], log_decay[0]]).reshape(2, n_ctx, hv_dev, seq).transpose(1, 0, 2, 3)
    )
    hi = lax.reduce_precision(rates_decay, exponent_bits=8, mantissa_bits=7)
    rest = rates_decay - hi
    mid = lax.reduce_precision(rest, exponent_bits=8, mantissa_bits=7)
    lo = lax.reduce_precision(rest - mid, exponent_bits=8, mantissa_bits=7)
    parts = jnp.stack([hi, mid, lo], axis=1).astype(jnp.bfloat16).reshape(n_ctx, 1, -1)
    width = 2 * qw + 2 * vw
    packed = jnp.concatenate(
        [
            jnp.concatenate(
                [
                    queries[0].reshape(seq, n_ctx, qw),
                    keys[0].reshape(seq, n_ctx, qw),
                    values[0].reshape(seq, n_ctx, vw),
                    gate_input[0].reshape(seq, n_ctx, vw),
                ],
                axis=2,
            ).transpose(1, 0, 2),
            jnp.pad(parts, ((0, 0), (0, 0), (0, width - parts.shape[-1]))),
        ],
        axis=1,
    )
    got = lax.all_to_all(packed, "ctx", 0, 0, tiled=True)
    arrived = got[:, :seq]
    rd = (
        got[:, seq, : parts.shape[-1]]
        .astype(jnp.float32)
        .reshape(n_ctx, 3, 2, hv_dev, seq)
    )
    rd = (rd[:, 0] + rd[:, 1]) + rd[:, 2]
    rates = rd[:, 0].transpose(1, 0, 2)
    gamma = jnp.cumsum(rd[:, 1].transpose(1, 0, 2), axis=-1)
    qc = unit_rows(arrived[..., :qw]) * DK ** (-0.5)
    kc = unit_rows(arrived[..., qw : 2 * qw])
    vc = (
        arrived[..., 2 * qw : 2 * qw + vw]
        .astype(jnp.float32)
        .reshape(n_ctx, seq, hv_dev, DV)
        .transpose(2, 0, 1, 3)
    )
    gc = arrived[..., 2 * qw + vw :].reshape(n_ctx, seq, hv_dev, DV)

    ordinals = jnp.arange(seq)
    before = ordinals[:, None] > ordinals[None, :]
    upto = ordinals[:, None] >= ordinals[None, :]
    spans = gamma[..., :, None] - gamma[..., None, :]
    pair_decay = jnp.exp(jnp.where(upto, spans, 0.0))
    key_key = jnp.einsum("ntd,nsd->nts", kc, kc, precision=highest)
    lower = jnp.where(before, pair_decay * key_key[None] * rates[..., None, :], 0.0)
    inverse = unit_lower_inverse(lower)
    growth = jnp.exp(gamma)
    right = jnp.concatenate(
        [vc, growth[..., None] * jnp.broadcast_to(kc[None], vc.shape)], axis=-1
    )
    solved = jnp.einsum("hnts,hnsf->hntf", inverse, right, precision=highest)
    solved_values = solved[..., :DV]
    solved_keys = solved[..., DV:]
    tail = rates * jnp.exp(gamma[..., -1:] - gamma)
    weighted = (kc[None] * tail[..., None]).reshape(hv_dev * n_ctx, seq, DK)
    carried = jnp.einsum(
        "btd,btf->bdf", weighted, solved.reshape(hv_dev * n_ctx, seq, DV + DK), precision=highest
    ).reshape(hv_dev, n_ctx, DK, DV + DK)
    identity = jnp.eye(DK, dtype=jnp.float32)
    transfer = growth[..., -1, None, None] * identity - carried[..., DV:]
    offset = carried[..., :DV]
    state = jnp.zeros((hv_dev, DK, DV), jnp.float32)
    states = [state]
    for n in range(n_ctx - 1):
        state = offset[:, n] + jnp.einsum(
            "hde,hef->hdf", transfer[:, n], state, precision=highest
        )
        states.append(state)
    states = jnp.stack(states, axis=1)
    pseudo = solved_values - jnp.einsum("hntd,hnde->hnte", solved_keys, states, precision=highest)
    query_key = jnp.einsum("ntd,nsd->nts", qc, kc, precision=highest)
    mixing = jnp.where(upto, pair_decay * query_key[None] * rates[..., None, :], 0.0)
    core = growth[..., None] * jnp.einsum("ntd,hnde->hnte", qc, states, precision=highest)
    core = core + jnp.einsum("hnts,hnse->hnte", mixing, pseudo, precision=highest)

    last = accepted[0] - 1
    chunk = last // seq
    local = last % seq
    gamma_chunk = lax.dynamic_index_in_dim(gamma, chunk, axis=1, keepdims=False)
    rates_chunk = lax.dynamic_index_in_dim(rates, chunk, axis=1, keepdims=False)
    pseudo_chunk = lax.dynamic_index_in_dim(pseudo, chunk, axis=1, keepdims=False)
    state_chunk = lax.dynamic_index_in_dim(states, chunk, axis=1, keepdims=False)
    keys_chunk = lax.dynamic_index_in_dim(kc, chunk, axis=0, keepdims=False)
    gamma_at = lax.dynamic_index_in_dim(gamma_chunk, local, axis=1, keepdims=False)
    keep = jnp.where(
        ordinals[None, :] <= local,
        rates_chunk * jnp.exp(jnp.minimum(gamma_at[:, None] - gamma_chunk, 0.0)),
        0.0,
    )
    final_state = jnp.exp(gamma_at)[:, None, None] * state_chunk + jnp.einsum(
        "td,hte->hde", keys_chunk, keep[..., None] * pseudo_chunk, precision=highest
    )
    final_state = final_state[None]

    scale = lax.rsqrt(jnp.mean(core * core, axis=-1, keepdims=True) + 1e-06)
    gating = jax.nn.silu(gc.astype(jnp.float32).transpose(2, 0, 1, 3))
    normed = (core * scale * norm_gain * gating).astype(jnp.bfloat16)
    normed = normed.transpose(1, 2, 0, 3).reshape(n_ctx, seq, vw)
    back = lax.all_to_all(normed, "ctx", 0, 0, tiled=True)
    resid = hidden[0].astype(jnp.float32) + jnp.einsum(
        "jtf,jfd->td",
        back,
        w_out.reshape(n_ctx, vw, D),
        preferred_element_type=jnp.float32,
    )
    moe_in = (
        resid * lax.rsqrt(jnp.mean(resid * resid, axis=-1, keepdims=True) + 1e-06) * post_gain
    ).astype(jnp.bfloat16)

    flat_ids = routes[0].reshape(-1)
    onehot = (flat_ids[:, None] == jnp.arange(experts, dtype=jnp.int32)[None, :]).astype(jnp.int32)
    earlier = jnp.cumsum(onehot, axis=0) - onehot
    slot = jnp.sum(earlier * onehot, axis=1)
    target = (flat_ids * cap + slot).reshape(seq, TOPK)
    slots = (
        jnp.arange(experts * cap, dtype=jnp.int32)
        .reshape(n_dev, EXP_DEV, cap)
        .transpose(0, 2, 1)
    )
    hits = target[None, None, None, :, :] == slots[..., None, None]
    dispatch = jnp.sum(jnp.where(hits, 1.0, 0.0), axis=-1).astype(jnp.bfloat16)
    outgoing_rows = jnp.einsum(
        "dcet,tf->dcef", dispatch, moe_in, preferred_element_type=jnp.float32
    ).astype(jnp.bfloat16)
    arrived_rows = lax.all_to_all(
        outgoing_rows, ("ctx", "req"), split_axis=0, concat_axis=0, tiled=True
    )
    both = jnp.einsum(
        "scex,exf->escf", arrived_rows, expert_gate_up, preferred_element_type=jnp.float32
    )
    inner = (jax.nn.silu(both[..., :FFE]) * both[..., FFE:]).astype(jnp.bfloat16)
    result = jnp.einsum(
        "escf,efx->scex", inner, expert_down, preferred_element_type=jnp.float32
    ).astype(jnp.bfloat16)
    returned = lax.all_to_all(result, ("ctx", "req"), split_axis=0, concat_axis=0, tiled=True)
    scores = route_scores[0]
    mix_weights = scores / jnp.sum(scores, axis=-1, keepdims=True)
    combine = jnp.sum(jnp.where(hits, mix_weights, 0.0), axis=-1)
    combine_hi = lax.reduce_precision(combine, exponent_bits=8, mantissa_bits=7)
    combine_lo = combine - combine_hi
    halves = jnp.concatenate([combine_hi, combine_lo], axis=-1).astype(jnp.bfloat16)
    both_out = jnp.einsum(
        "dcet,dcex->tx", halves, returned, preferred_element_type=jnp.float32
    )
    moe_out = both_out[:seq] + both_out[seq:]
    layer_out = (resid + moe_out).astype(jnp.bfloat16)[None]
    return (layer_out, final_state)


def solution(mesh):
    placed = (
        P("req", "ctx", None),
        P("req", "ctx", None),
        P("req", "ctx", None),
        P("req", "ctx", None),
        P("req", None, "ctx"),
        P("req", None, "ctx"),
        P(),
        P(),
        P("req", "ctx", None),
        P(),
        P("req", "ctx", None),
        P("req", "ctx", None),
        P(("ctx", "req"), None, None),
        P(("ctx", "req"), None, None),
        P("req"),
    )
    return jax.shard_map(
        shards,
        mesh=mesh,
        in_specs=placed,
        out_specs=(P("req", "ctx", None), P("req", "ctx", None, None)),
        check_vma=False,
    )
```

```python
import jax
import jax.numpy as jnp
from jax import lax
from jax.sharding import PartitionSpec as P

D = 2048
HK = 8
HV = 16
DK = 128
DV = 128
FFE = 512
TOPK = 10
EXP_DEV = 2


def unit_rows(x):
    x = x.astype(jnp.float32)
    return x * lax.rsqrt(jnp.sum(x * x, axis=-1, keepdims=True) + 1e-06)


def unit_lower_inverse(lower):
    highest = lax.Precision.HIGHEST
    n = lower.shape[-1]
    rows = jnp.arange(n)[:, None]
    cols = jnp.arange(n)[None, :]
    inv = None
    b = 1
    while b < n:
        sel = (rows // (2 * b) == cols // (2 * b)) & ((rows // b) % 2 == 1) & ((cols // b) % 2 == 0)
        c = jnp.where(sel, lower, 0.0)
        if inv is None:
            inv = lax.optimization_barrier(jnp.eye(n, dtype=lower.dtype) - c)
        else:
            mc = jnp.einsum("...ij,...jk->...ik", inv, c, precision=highest)
            inv = inv - jnp.einsum("...ij,...jk->...ik", mc, inv, precision=highest)
        b *= 2
    return inv


def run_experts(arrived, expert_gate_up, expert_down):
    provider_rows, count, part, width = arrived.shape
    rows = arrived.transpose(1, 0, 2, 3).reshape(count, provider_rows * part, width)
    both = jnp.einsum("erd,edf->erf", rows, expert_gate_up, preferred_element_type=jnp.float32)
    inner = (jax.nn.silu(both[..., :FFE]) * both[..., FFE:]).astype(jnp.bfloat16)
    result = jnp.einsum(
        "erf,efd->erd", inner, expert_down, preferred_element_type=jnp.float32
    ).astype(jnp.bfloat16)
    return result.reshape(count, provider_rows, part, width).transpose(1, 0, 2, 3)


def shards(
    queries,
    keys,
    values,
    gate_input,
    beta,
    log_decay,
    norm_gain,
    w_out,
    hidden,
    post_gain,
    routes,
    route_scores,
    expert_gate_up,
    expert_down,
    accepted,
):
    highest = lax.Precision.HIGHEST
    seq = queries.shape[1]
    n_ctx = lax.axis_size("ctx")
    n_req = lax.axis_size("req")
    n_dev = n_ctx * n_req
    experts = EXP_DEV * n_dev
    cap = max(2, 3 * seq * TOPK // (2 * experts))
    kh_dev = HK // n_ctx
    hv_dev = HV // n_ctx
    qw = kh_dev * DK
    vw = hv_dev * DV

    rates_decay = (
        jnp.stack([beta[0], log_decay[0]]).reshape(2, n_ctx, hv_dev, seq).transpose(1, 0, 2, 3)
    )
    hi = lax.reduce_precision(rates_decay, exponent_bits=8, mantissa_bits=7)
    rest = rates_decay - hi
    mid = lax.reduce_precision(rest, exponent_bits=8, mantissa_bits=7)
    lo = lax.reduce_precision(rest - mid, exponent_bits=8, mantissa_bits=7)
    parts = jnp.stack([hi, mid, lo], axis=1).astype(jnp.bfloat16).reshape(n_ctx, 1, -1)
    width = 2 * qw + 2 * vw
    packed = jnp.concatenate(
        [
            jnp.concatenate(
                [
                    queries[0].reshape(seq, n_ctx, qw),
                    keys[0].reshape(seq, n_ctx, qw),
                    values[0].reshape(seq, n_ctx, vw),
                    gate_input[0].reshape(seq, n_ctx, vw),
                ],
                axis=2,
            ).transpose(1, 0, 2),
            jnp.pad(parts, ((0, 0), (0, 0), (0, width - parts.shape[-1]))),
        ],
        axis=1,
    )
    got = lax.all_to_all(packed, "ctx", 0, 0, tiled=True)
    arrived = got[:, :seq]
    rd = (
        got[:, seq, : parts.shape[-1]]
        .astype(jnp.float32)
        .reshape(n_ctx, 3, 2, hv_dev, seq)
    )
    rd = (rd[:, 0] + rd[:, 1]) + rd[:, 2]
    rates = rd[:, 0].transpose(1, 0, 2)
    gamma = jnp.cumsum(rd[:, 1].transpose(1, 0, 2), axis=-1)
    qc = unit_rows(arrived[..., :qw]) * DK ** (-0.5)
    kc = unit_rows(arrived[..., qw : 2 * qw])
    vc = (
        arrived[..., 2 * qw : 2 * qw + vw]
        .astype(jnp.float32)
        .reshape(n_ctx, seq, hv_dev, DV)
        .transpose(2, 0, 1, 3)
    )
    gc = arrived[..., 2 * qw + vw :].reshape(n_ctx, seq, hv_dev, DV)

    ordinals = jnp.arange(seq)
    before = ordinals[:, None] > ordinals[None, :]
    upto = ordinals[:, None] >= ordinals[None, :]
    spans = gamma[..., :, None] - gamma[..., None, :]
    pair_decay = jnp.exp(jnp.where(upto, spans, 0.0))
    key_key = jnp.einsum("ntd,nsd->nts", kc, kc, precision=highest)
    lower = jnp.where(before, pair_decay * key_key[None] * rates[..., None, :], 0.0)
    inverse = unit_lower_inverse(lower)
    growth = jnp.exp(gamma)
    right = jnp.concatenate(
        [vc, growth[..., None] * jnp.broadcast_to(kc[None], vc.shape)], axis=-1
    )
    solved = jnp.einsum("hnts,hnsf->hntf", inverse, right, precision=highest)
    solved_values = solved[..., :DV]
    solved_keys = solved[..., DV:]
    tail = rates * jnp.exp(gamma[..., -1:] - gamma)
    weighted = (kc[None] * tail[..., None]).reshape(hv_dev * n_ctx, seq, DK)
    carried = jnp.einsum(
        "btd,btf->bdf", weighted, solved.reshape(hv_dev * n_ctx, seq, DV + DK), precision=highest
    ).reshape(hv_dev, n_ctx, DK, DV + DK)
    identity = jnp.eye(DK, dtype=jnp.float32)
    transfer = growth[..., -1, None, None] * identity - carried[..., DV:]
    offset = carried[..., :DV]
    state = jnp.zeros((hv_dev, DK, DV), jnp.float32)
    states = [state]
    for n in range(n_ctx - 1):
        state = offset[:, n] + jnp.einsum(
            "hde,hef->hdf", transfer[:, n], state, precision=highest
        )
        states.append(state)
    states = jnp.stack(states, axis=1)
    pseudo = solved_values - jnp.einsum("hntd,hnde->hnte", solved_keys, states, precision=highest)
    query_key = jnp.einsum("ntd,nsd->nts", qc, kc, precision=highest)
    mixing = jnp.where(upto, pair_decay * query_key[None] * rates[..., None, :], 0.0)
    core = growth[..., None] * jnp.einsum("ntd,hnde->hnte", qc, states, precision=highest)
    core = core + jnp.einsum("hnts,hnse->hnte", mixing, pseudo, precision=highest)

    last = accepted[0] - 1
    chunk = last // seq
    local = last % seq
    gamma_chunk = lax.dynamic_index_in_dim(gamma, chunk, axis=1, keepdims=False)
    rates_chunk = lax.dynamic_index_in_dim(rates, chunk, axis=1, keepdims=False)
    pseudo_chunk = lax.dynamic_index_in_dim(pseudo, chunk, axis=1, keepdims=False)
    state_chunk = lax.dynamic_index_in_dim(states, chunk, axis=1, keepdims=False)
    keys_chunk = lax.dynamic_index_in_dim(kc, chunk, axis=0, keepdims=False)
    gamma_at = lax.dynamic_index_in_dim(gamma_chunk, local, axis=1, keepdims=False)
    keep = jnp.where(
        ordinals[None, :] <= local,
        rates_chunk * jnp.exp(jnp.minimum(gamma_at[:, None] - gamma_chunk, 0.0)),
        0.0,
    )
    final_state = jnp.exp(gamma_at)[:, None, None] * state_chunk + jnp.einsum(
        "td,hte->hde", keys_chunk, keep[..., None] * pseudo_chunk, precision=highest
    )
    final_state = final_state[None]

    scale = lax.rsqrt(jnp.mean(core * core, axis=-1, keepdims=True) + 1e-06)
    gating = jax.nn.silu(gc.astype(jnp.float32).transpose(2, 0, 1, 3))
    normed = (core * scale * norm_gain * gating).astype(jnp.bfloat16)
    normed = normed.transpose(1, 2, 0, 3).reshape(n_ctx, seq, vw)
    back = lax.all_to_all(normed, "ctx", 0, 0, tiled=True)
    resid = hidden[0].astype(jnp.float32) + jnp.einsum(
        "jtf,jfd->td",
        back,
        w_out.reshape(n_ctx, vw, D),
        preferred_element_type=jnp.float32,
    )
    moe_in = (
        resid * lax.rsqrt(jnp.mean(resid * resid, axis=-1, keepdims=True) + 1e-06) * post_gain
    ).astype(jnp.bfloat16)

    flat_ids = routes[0].reshape(-1)
    onehot = (flat_ids[:, None] == jnp.arange(experts, dtype=jnp.int32)[None, :]).astype(jnp.int32)
    earlier = jnp.cumsum(onehot, axis=0) - onehot
    slot = jnp.sum(earlier * onehot, axis=1)
    target = (flat_ids * cap + slot).reshape(seq, TOPK)
    slots = (
        jnp.arange(experts * cap, dtype=jnp.int32)
        .reshape(n_dev, EXP_DEV, cap)
        .transpose(0, 2, 1)
    )
    hits = target[None, None, None, :, :] == slots[..., None, None]
    dispatch = jnp.sum(jnp.where(hits, 1.0, 0.0), axis=-1).astype(jnp.bfloat16)
    outgoing_rows = jnp.dot(
        dispatch.reshape(experts * cap, seq), moe_in, preferred_element_type=jnp.float32
    ).astype(jnp.bfloat16)
    arrived_rows = lax.all_to_all(
        outgoing_rows, ("ctx", "req"), split_axis=0, concat_axis=0, tiled=True
    ).reshape(n_dev, cap, EXP_DEV, D)
    both = jnp.einsum(
        "scex,exf->escf", arrived_rows, expert_gate_up, preferred_element_type=jnp.float32
    )
    inner = (jax.nn.silu(both[..., :FFE]) * both[..., FFE:]).astype(jnp.bfloat16)
    result = jnp.einsum(
        "escf,efx->scex", inner, expert_down, preferred_element_type=jnp.float32
    ).astype(jnp.bfloat16)
    returned = lax.all_to_all(
        result.reshape(experts * cap, D), ("ctx", "req"), split_axis=0, concat_axis=0, tiled=True
    ).reshape(n_dev, cap, EXP_DEV, D)
    scores = route_scores[0]
    mix_weights = scores / jnp.sum(scores, axis=-1, keepdims=True)
    combine = jnp.sum(jnp.where(hits, mix_weights, 0.0), axis=-1)
    combine_hi = lax.reduce_precision(combine, exponent_bits=8, mantissa_bits=7)
    combine_lo = combine - combine_hi
    halves = jnp.concatenate([combine_hi, combine_lo], axis=-1).astype(jnp.bfloat16)
    both_out = jnp.einsum(
        "dcet,dcex->tx", halves, returned, preferred_element_type=jnp.float32
    )
    moe_out = both_out[:seq] + both_out[seq:]
    layer_out = (resid + moe_out).astype(jnp.bfloat16)[None]
    return (layer_out, final_state)


def solution(mesh):
    placed = (
        P("req", "ctx", None),
        P("req", "ctx", None),
        P("req", "ctx", None),
        P("req", "ctx", None),
        P("req", None, "ctx"),
        P("req", None, "ctx"),
        P(),
        P(),
        P("req", "ctx", None),
        P(),
        P("req", "ctx", None),
        P("req", "ctx", None),
        P(("ctx", "req"), None, None),
        P(("ctx", "req"), None, None),
        P("req"),
    )
    return jax.shard_map(
        shards,
        mesh=mesh,
        in_specs=placed,
        out_specs=(P("req", "ctx", None), P("req", "ctx", None, None)),
        check_vma=False,
    )
```

```python
import jax
import jax.numpy as jnp
from jax import lax
from jax.sharding import PartitionSpec as P

D = 2048
HK = 8
HV = 16
DK = 128
DV = 128
FFE = 512
TOPK = 10
EXP_DEV = 2


def unit_rows(x):
    x = x.astype(jnp.float32)
    return x * lax.rsqrt(jnp.sum(x * x, axis=-1, keepdims=True) + 1e-06)


def unit_lower_inverse(lower):
    highest = lax.Precision.HIGHEST
    n = lower.shape[-1]
    rows = jnp.arange(n)[:, None]
    cols = jnp.arange(n)[None, :]
    inv = None
    b = 1
    while b < n:
        sel = (rows // (2 * b) == cols // (2 * b)) & ((rows // b) % 2 == 1) & ((cols // b) % 2 == 0)
        c = jnp.where(sel, lower, 0.0)
        if inv is None:
            inv = lax.optimization_barrier(jnp.eye(n, dtype=lower.dtype) - c)
        else:
            mc = jnp.einsum("...ij,...jk->...ik", inv, c, precision=highest)
            inv = inv - jnp.einsum("...ij,...jk->...ik", mc, inv, precision=highest)
        b *= 2
    return inv


def run_experts(arrived, expert_gate_up, expert_down):
    provider_rows, count, part, width = arrived.shape
    rows = arrived.transpose(1, 0, 2, 3).reshape(count, provider_rows * part, width)
    both = jnp.einsum("erd,edf->erf", rows, expert_gate_up, preferred_element_type=jnp.float32)
    inner = (jax.nn.silu(both[..., :FFE]) * both[..., FFE:]).astype(jnp.bfloat16)
    result = jnp.einsum(
        "erf,efd->erd", inner, expert_down, preferred_element_type=jnp.float32
    ).astype(jnp.bfloat16)
    return result.reshape(count, provider_rows, part, width).transpose(1, 0, 2, 3)


def shards(
    queries,
    keys,
    values,
    gate_input,
    beta,
    log_decay,
    norm_gain,
    w_out,
    hidden,
    post_gain,
    routes,
    route_scores,
    expert_gate_up,
    expert_down,
    accepted,
):
    highest = lax.Precision.HIGHEST
    seq = queries.shape[1]
    n_ctx = lax.axis_size("ctx")
    n_req = lax.axis_size("req")
    n_dev = n_ctx * n_req
    experts = EXP_DEV * n_dev
    cap = max(2, 3 * seq * TOPK // (2 * experts))
    kh_dev = HK // n_ctx
    hv_dev = HV // n_ctx
    qw = kh_dev * DK
    vw = hv_dev * DV

    rates_decay = (
        jnp.stack([beta[0], log_decay[0]]).reshape(2, n_ctx, hv_dev, seq).transpose(1, 0, 2, 3)
    )
    hi = lax.reduce_precision(rates_decay, exponent_bits=8, mantissa_bits=7)
    rest = rates_decay - hi
    mid = lax.reduce_precision(rest, exponent_bits=8, mantissa_bits=7)
    lo = lax.reduce_precision(rest - mid, exponent_bits=8, mantissa_bits=7)
    width = 2 * qw + vw
    parts = jnp.stack([hi, mid, lo], axis=1).astype(jnp.bfloat16).reshape(n_ctx, -1)
    extra = -(-parts.shape[-1] // width)
    parts = jnp.pad(parts, ((0, 0), (0, extra * width - parts.shape[-1]))).reshape(n_ctx, extra, width)
    packed = jnp.concatenate(
        [
            jnp.concatenate(
                [
                    queries[0].reshape(seq, n_ctx, qw),
                    keys[0].reshape(seq, n_ctx, qw),
                    values[0].reshape(seq, n_ctx, vw),
                ],
                axis=2,
            ).transpose(1, 0, 2),
            parts,
        ],
        axis=1,
    )
    got = lax.all_to_all(packed, "ctx", 0, 0, tiled=True)
    arrived = got[:, :seq]
    rd = (
        got[:, seq:]
        .reshape(n_ctx, -1)[:, : 3 * 2 * hv_dev * seq]
        .astype(jnp.float32)
        .reshape(n_ctx, 3, 2, hv_dev, seq)
    )
    rd = (rd[:, 0] + rd[:, 1]) + rd[:, 2]
    rates = rd[:, 0].transpose(1, 0, 2)
    gamma = jnp.cumsum(rd[:, 1].transpose(1, 0, 2), axis=-1)
    qc = unit_rows(arrived[..., :qw]) * DK ** (-0.5)
    kc = unit_rows(arrived[..., qw : 2 * qw])
    vc = (
        arrived[..., 2 * qw : 2 * qw + vw]
        .astype(jnp.float32)
        .reshape(n_ctx, seq, hv_dev, DV)
        .transpose(2, 0, 1, 3)
    )

    ordinals = jnp.arange(seq)
    before = ordinals[:, None] > ordinals[None, :]
    upto = ordinals[:, None] >= ordinals[None, :]
    spans = gamma[..., :, None] - gamma[..., None, :]
    pair_decay = jnp.exp(jnp.where(upto, spans, 0.0))
    key_key = jnp.einsum("ntd,nsd->nts", kc, kc, precision=highest)
    lower = jnp.where(before, pair_decay * key_key[None] * rates[..., None, :], 0.0)
    inverse = unit_lower_inverse(lower)
    growth = jnp.exp(gamma)
    right = jnp.concatenate(
        [vc, growth[..., None] * jnp.broadcast_to(kc[None], vc.shape)], axis=-1
    )
    solved = jnp.einsum("hnts,hnsf->hntf", inverse, right, precision=highest)
    solved_values = solved[..., :DV]
    solved_keys = solved[..., DV:]
    tail = rates * jnp.exp(gamma[..., -1:] - gamma)
    weighted = (kc[None] * tail[..., None]).reshape(hv_dev * n_ctx, seq, DK)
    carried = jnp.einsum(
        "btd,btf->bdf", weighted, solved.reshape(hv_dev * n_ctx, seq, DV + DK), precision=highest
    ).reshape(hv_dev, n_ctx, DK, DV + DK)
    identity = jnp.eye(DK, dtype=jnp.float32)
    transfer = growth[..., -1, None, None] * identity - carried[..., DV:]
    offset = carried[..., :DV]
    state = jnp.zeros((hv_dev, DK, DV), jnp.float32)
    states = [state]
    for n in range(n_ctx - 1):
        state = offset[:, n] + jnp.einsum(
            "hde,hef->hdf", transfer[:, n], state, precision=highest
        )
        states.append(state)
    states = jnp.stack(states, axis=1)
    pseudo = solved_values - jnp.einsum("hntd,hnde->hnte", solved_keys, states, precision=highest)
    query_key = jnp.einsum("ntd,nsd->nts", qc, kc, precision=highest)
    mixing = jnp.where(upto, pair_decay * query_key[None] * rates[..., None, :], 0.0)
    core = growth[..., None] * jnp.einsum("ntd,hnde->hnte", qc, states, precision=highest)
    core = core + jnp.einsum("hnts,hnse->hnte", mixing, pseudo, precision=highest)

    last = accepted[0] - 1
    chunk = last // seq
    local = last % seq
    gamma_chunk = lax.dynamic_index_in_dim(gamma, chunk, axis=1, keepdims=False)
    rates_chunk = lax.dynamic_index_in_dim(rates, chunk, axis=1, keepdims=False)
    pseudo_chunk = lax.dynamic_index_in_dim(pseudo, chunk, axis=1, keepdims=False)
    state_chunk = lax.dynamic_index_in_dim(states, chunk, axis=1, keepdims=False)
    keys_chunk = lax.dynamic_index_in_dim(kc, chunk, axis=0, keepdims=False)
    gamma_at = lax.dynamic_index_in_dim(gamma_chunk, local, axis=1, keepdims=False)
    keep = jnp.where(
        ordinals[None, :] <= local,
        rates_chunk * jnp.exp(jnp.minimum(gamma_at[:, None] - gamma_chunk, 0.0)),
        0.0,
    )
    final_state = jnp.exp(gamma_at)[:, None, None] * state_chunk + jnp.einsum(
        "td,hte->hde", keys_chunk, keep[..., None] * pseudo_chunk, precision=highest
    )
    final_state = final_state[None]

    scale = lax.rsqrt(jnp.mean(core * core, axis=-1, keepdims=True) + 1e-06)
    shaped = (core * scale * norm_gain).astype(jnp.bfloat16)
    shaped = shaped.transpose(1, 2, 0, 3).reshape(n_ctx, seq, vw)
    back = lax.all_to_all(shaped, "ctx", 0, 0, tiled=True)
    gating = jax.nn.silu(gate_input[0].astype(jnp.float32).reshape(seq, n_ctx, vw).transpose(1, 0, 2))
    normed = (back.astype(jnp.float32) * gating).astype(jnp.bfloat16)
    resid = hidden[0].astype(jnp.float32) + jnp.einsum(
        "jtf,jfd->td",
        normed,
        w_out.reshape(n_ctx, vw, D),
        preferred_element_type=jnp.float32,
    )
    moe_in = (
        resid * lax.rsqrt(jnp.mean(resid * resid, axis=-1, keepdims=True) + 1e-06) * post_gain
    ).astype(jnp.bfloat16)

    flat_ids = routes[0].reshape(-1)
    onehot = (flat_ids[:, None] == jnp.arange(experts, dtype=jnp.int32)[None, :]).astype(jnp.int32)
    earlier = jnp.cumsum(onehot, axis=0) - onehot
    slot = jnp.sum(earlier * onehot, axis=1)
    target = (flat_ids * cap + slot).reshape(seq, TOPK)
    slots = (
        jnp.arange(experts * cap, dtype=jnp.int32)
        .reshape(n_dev, EXP_DEV, cap)
        .transpose(0, 2, 1)
    )
    hits = target[None, None, None, :, :] == slots[..., None, None]
    dispatch = jnp.sum(jnp.where(hits, 1.0, 0.0), axis=-1).astype(jnp.bfloat16)
    outgoing_rows = jnp.einsum(
        "dcet,tf->dcef", dispatch, moe_in, preferred_element_type=jnp.float32
    ).astype(jnp.bfloat16)
    arrived_rows = lax.all_to_all(
        outgoing_rows, ("ctx", "req"), split_axis=0, concat_axis=0, tiled=True
    )
    both = jnp.einsum(
        "scex,exf->escf", arrived_rows, expert_gate_up, preferred_element_type=jnp.float32
    )
    inner = (jax.nn.silu(both[..., :FFE]) * both[..., FFE:]).astype(jnp.bfloat16)
    result = jnp.einsum(
        "escf,efx->scex", inner, expert_down, preferred_element_type=jnp.float32
    ).astype(jnp.bfloat16)
    returned = lax.all_to_all(result, ("ctx", "req"), split_axis=0, concat_axis=0, tiled=True)
    scores = route_scores[0]
    mix_weights = scores / jnp.sum(scores, axis=-1, keepdims=True)
    combine = jnp.sum(jnp.where(hits, mix_weights, 0.0), axis=-1)
    combine_hi = lax.reduce_precision(combine, exponent_bits=8, mantissa_bits=7)
    combine_lo = combine - combine_hi
    halves = jnp.concatenate([combine_hi, combine_lo], axis=-1).astype(jnp.bfloat16)
    both_out = jnp.einsum(
        "dcet,dcex->tx", halves, returned, preferred_element_type=jnp.float32
    )
    moe_out = both_out[:seq] + both_out[seq:]
    layer_out = (resid + moe_out).astype(jnp.bfloat16)[None]
    return (layer_out, final_state)


def solution(mesh):
    placed = (
        P("req", "ctx", None),
        P("req", "ctx", None),
        P("req", "ctx", None),
        P("req", "ctx", None),
        P("req", None, "ctx"),
        P("req", None, "ctx"),
        P(),
        P(),
        P("req", "ctx", None),
        P(),
        P("req", "ctx", None),
        P("req", "ctx", None),
        P(("ctx", "req"), None, None),
        P(("ctx", "req"), None, None),
        P("req"),
    )
    return jax.shard_map(
        shards,
        mesh=mesh,
        in_specs=placed,
        out_specs=(P("req", "ctx", None), P("req", "ctx", None, None)),
        check_vma=False,
    )
```

```python
import jax
import jax.numpy as jnp
from jax import lax
from jax.sharding import PartitionSpec as P

D = 2048
HK = 8
HV = 16
DK = 128
DV = 128
FFE = 512
TOPK = 10
EXP_DEV = 2


def unit_rows(x):
    x = x.astype(jnp.float32)
    return x * lax.rsqrt(jnp.sum(x * x, axis=-1, keepdims=True) + 1e-06)


def unit_lower_inverse(lower):
    highest = lax.Precision.HIGHEST
    n = lower.shape[-1]
    rows = jnp.arange(n)[:, None]
    cols = jnp.arange(n)[None, :]
    inv = None
    b = 1
    while b < n:
        sel = (rows // (2 * b) == cols // (2 * b)) & ((rows // b) % 2 == 1) & ((cols // b) % 2 == 0)
        c = jnp.where(sel, lower, 0.0)
        if inv is None:
            inv = lax.optimization_barrier(jnp.eye(n, dtype=lower.dtype) - c)
        else:
            mc = jnp.einsum("...ij,...jk->...ik", inv, c, precision=highest)
            inv = inv - jnp.einsum("...ij,...jk->...ik", mc, inv, precision=highest)
        b *= 2
    return inv


def run_experts(arrived, expert_gate_up, expert_down):
    provider_rows, count, part, width = arrived.shape
    rows = arrived.transpose(1, 0, 2, 3).reshape(count, provider_rows * part, width)
    both = jnp.einsum("erd,edf->erf", rows, expert_gate_up, preferred_element_type=jnp.float32)
    inner = (jax.nn.silu(both[..., :FFE]) * both[..., FFE:]).astype(jnp.bfloat16)
    result = jnp.einsum(
        "erf,efd->erd", inner, expert_down, preferred_element_type=jnp.float32
    ).astype(jnp.bfloat16)
    return result.reshape(count, provider_rows, part, width).transpose(1, 0, 2, 3)


def shards(
    queries,
    keys,
    values,
    gate_input,
    beta,
    log_decay,
    norm_gain,
    w_out,
    hidden,
    post_gain,
    routes,
    route_scores,
    expert_gate_up,
    expert_down,
    accepted,
):
    highest = lax.Precision.HIGHEST
    seq = queries.shape[1]
    n_ctx = lax.axis_size("ctx")
    n_req = lax.axis_size("req")
    n_dev = n_ctx * n_req
    experts = EXP_DEV * n_dev
    cap = max(2, 3 * seq * TOPK // (2 * experts))
    kh_dev = HK // n_ctx
    hv_dev = HV // n_ctx
    qw = kh_dev * DK
    vw = hv_dev * DV

    rates_decay = (
        jnp.stack([beta[0], log_decay[0]]).reshape(2, n_ctx, hv_dev, seq).transpose(1, 0, 2, 3)
    )
    hi = lax.reduce_precision(rates_decay, exponent_bits=8, mantissa_bits=7)
    rest = rates_decay - hi
    mid = lax.reduce_precision(rest, exponent_bits=8, mantissa_bits=7)
    lo = lax.reduce_precision(rest - mid, exponent_bits=8, mantissa_bits=7)
    width = 2 * qw + vw
    parts = jnp.stack([hi, mid, lo], axis=1).astype(jnp.bfloat16).reshape(n_ctx, -1)
    extra = -(-parts.shape[-1] // width)
    parts = jnp.pad(parts, ((0, 0), (0, extra * width - parts.shape[-1]))).reshape(n_ctx, extra, width)
    packed = jnp.concatenate(
        [
            jnp.concatenate(
                [
                    queries[0].reshape(seq, n_ctx, qw),
                    keys[0].reshape(seq, n_ctx, qw),
                    values[0].reshape(seq, n_ctx, vw),
                ],
                axis=2,
            ).transpose(1, 0, 2),
            parts,
        ],
        axis=1,
    )
    got = lax.all_to_all(packed, "ctx", 0, 0, tiled=True)
    arrived = got[:, :seq]
    rd = (
        got[:, seq:]
        .reshape(n_ctx, -1)[:, : 3 * 2 * hv_dev * seq]
        .astype(jnp.float32)
        .reshape(n_ctx, 3, 2, hv_dev, seq)
    )
    rd = (rd[:, 0] + rd[:, 1]) + rd[:, 2]
    rates = rd[:, 0].transpose(1, 0, 2)
    gamma = jnp.cumsum(rd[:, 1].transpose(1, 0, 2), axis=-1)
    qc = unit_rows(arrived[..., :qw]) * DK ** (-0.5)
    kc = unit_rows(arrived[..., qw : 2 * qw])
    vc = (
        arrived[..., 2 * qw : 2 * qw + vw]
        .astype(jnp.float32)
        .reshape(n_ctx, seq, hv_dev, DV)
        .transpose(2, 0, 1, 3)
    )

    ordinals = jnp.arange(seq)
    before = ordinals[:, None] > ordinals[None, :]
    upto = ordinals[:, None] >= ordinals[None, :]
    spans = gamma[..., :, None] - gamma[..., None, :]
    pair_decay = jnp.exp(jnp.where(upto, spans, 0.0))
    key_key = jnp.einsum("ntd,nsd->nts", kc, kc, precision=highest)
    lower = jnp.where(before, pair_decay * key_key[None] * rates[..., None, :], 0.0)
    inverse = unit_lower_inverse(lower)
    growth = jnp.exp(gamma)
    right = jnp.concatenate(
        [vc, growth[..., None] * jnp.broadcast_to(kc[None], vc.shape)], axis=-1
    )
    solved = jnp.einsum("hnts,hnsf->hntf", inverse, right, precision=highest)
    solved_values = solved[..., :DV]
    solved_keys = solved[..., DV:]
    tail = rates * jnp.exp(gamma[..., -1:] - gamma)
    weighted = (kc[None] * tail[..., None]).reshape(hv_dev * n_ctx, seq, DK)
    carried = jnp.einsum(
        "btd,btf->bdf", weighted, solved.reshape(hv_dev * n_ctx, seq, DV + DK), precision=highest
    ).reshape(hv_dev, n_ctx, DK, DV + DK)
    growth_last = growth[..., -1]
    key_part = carried[..., DV:]
    offset = carried[..., :DV]
    state = jnp.zeros((hv_dev, DK, DV), jnp.float32)
    states = [state]
    for n in range(n_ctx - 1):
        state = (
            offset[:, n]
            + growth_last[:, n, None, None] * state
            - jnp.einsum("hde,hef->hdf", key_part[:, n], state, precision=highest)
        )
        states.append(state)
    states = jnp.stack(states, axis=1)
    pseudo = solved_values - jnp.einsum("hntd,hnde->hnte", solved_keys, states, precision=highest)
    query_key = jnp.einsum("ntd,nsd->nts", qc, kc, precision=highest)
    mixing = jnp.where(upto, pair_decay * query_key[None] * rates[..., None, :], 0.0)
    core = growth[..., None] * jnp.einsum("ntd,hnde->hnte", qc, states, precision=highest)
    core = core + jnp.einsum("hnts,hnse->hnte", mixing, pseudo, precision=highest)

    last = accepted[0] - 1
    chunk = last // seq
    local = last % seq
    gamma_chunk = lax.dynamic_index_in_dim(gamma, chunk, axis=1, keepdims=False)
    rates_chunk = lax.dynamic_index_in_dim(rates, chunk, axis=1, keepdims=False)
    pseudo_chunk = lax.dynamic_index_in_dim(pseudo, chunk, axis=1, keepdims=False)
    state_chunk = lax.dynamic_index_in_dim(states, chunk, axis=1, keepdims=False)
    keys_chunk = lax.dynamic_index_in_dim(kc, chunk, axis=0, keepdims=False)
    gamma_at = lax.dynamic_index_in_dim(gamma_chunk, local, axis=1, keepdims=False)
    keep = jnp.where(
        ordinals[None, :] <= local,
        rates_chunk * jnp.exp(jnp.minimum(gamma_at[:, None] - gamma_chunk, 0.0)),
        0.0,
    )
    final_state = jnp.exp(gamma_at)[:, None, None] * state_chunk + jnp.einsum(
        "td,hte->hde", keys_chunk, keep[..., None] * pseudo_chunk, precision=highest
    )
    final_state = final_state[None]

    scale = lax.rsqrt(jnp.mean(core * core, axis=-1, keepdims=True) + 1e-06)
    shaped = (core * scale * norm_gain).astype(jnp.bfloat16)
    shaped = shaped.transpose(1, 2, 0, 3).reshape(n_ctx, seq, vw)
    back = lax.all_to_all(shaped, "ctx", 0, 0, tiled=True)
    gating = jax.nn.silu(gate_input[0].astype(jnp.float32).reshape(seq, n_ctx, vw).transpose(1, 0, 2))
    normed = (back.astype(jnp.float32) * gating).astype(jnp.bfloat16)
    resid = hidden[0].astype(jnp.float32) + jnp.einsum(
        "jtf,jfd->td",
        normed,
        w_out.reshape(n_ctx, vw, D),
        preferred_element_type=jnp.float32,
    )
    moe_in = (
        resid * lax.rsqrt(jnp.mean(resid * resid, axis=-1, keepdims=True) + 1e-06) * post_gain
    ).astype(jnp.bfloat16)

    flat_ids = routes[0].reshape(-1)
    onehot = (flat_ids[:, None] == jnp.arange(experts, dtype=jnp.int32)[None, :]).astype(jnp.int32)
    earlier = jnp.cumsum(onehot, axis=0) - onehot
    slot = jnp.sum(earlier * onehot, axis=1)
    target = (flat_ids * cap + slot).reshape(seq, TOPK)
    slots = (
        jnp.arange(experts * cap, dtype=jnp.int32)
        .reshape(n_dev, EXP_DEV, cap)
        .transpose(0, 2, 1)
    )
    hits = target[None, None, None, :, :] == slots[..., None, None]
    dispatch = jnp.sum(jnp.where(hits, 1.0, 0.0), axis=-1).astype(jnp.bfloat16)
    outgoing_rows = jnp.einsum(
        "dcet,tf->dcef", dispatch, moe_in, preferred_element_type=jnp.float32
    ).astype(jnp.bfloat16)
    arrived_rows = lax.all_to_all(
        outgoing_rows, ("ctx", "req"), split_axis=0, concat_axis=0, tiled=True
    )
    both = jnp.einsum(
        "scex,exf->escf", arrived_rows, expert_gate_up, preferred_element_type=jnp.float32
    )
    inner = (jax.nn.silu(both[..., :FFE]) * both[..., FFE:]).astype(jnp.bfloat16)
    result = jnp.einsum(
        "escf,efx->scex", inner, expert_down, preferred_element_type=jnp.float32
    ).astype(jnp.bfloat16)
    returned = lax.all_to_all(result, ("ctx", "req"), split_axis=0, concat_axis=0, tiled=True)
    scores = route_scores[0]
    mix_weights = scores / jnp.sum(scores, axis=-1, keepdims=True)
    combine = jnp.sum(jnp.where(hits, mix_weights, 0.0), axis=-1)
    combine_hi = lax.reduce_precision(combine, exponent_bits=8, mantissa_bits=7)
    combine_lo = combine - combine_hi
    halves = jnp.concatenate([combine_hi, combine_lo], axis=-1).astype(jnp.bfloat16)
    both_out = jnp.einsum(
        "dcet,dcex->tx", halves, returned, preferred_element_type=jnp.float32
    )
    moe_out = both_out[:seq] + both_out[seq:]
    layer_out = (resid + moe_out).astype(jnp.bfloat16)[None]
    return (layer_out, final_state)


def solution(mesh):
    placed = (
        P("req", "ctx", None),
        P("req", "ctx", None),
        P("req", "ctx", None),
        P("req", "ctx", None),
        P("req", None, "ctx"),
        P("req", None, "ctx"),
        P(),
        P(),
        P("req", "ctx", None),
        P(),
        P("req", "ctx", None),
        P("req", "ctx", None),
        P(("ctx", "req"), None, None),
        P(("ctx", "req"), None, None),
        P("req"),
    )
    return jax.shard_map(
        shards,
        mesh=mesh,
        in_specs=placed,
        out_specs=(P("req", "ctx", None), P("req", "ctx", None, None)),
        check_vma=False,
    )
```

```python
import jax
import jax.numpy as jnp
from jax import lax
from jax.sharding import PartitionSpec as P

D = 2048
HK = 8
HV = 16
DK = 128
DV = 128
FFE = 512
TOPK = 10
EXP_DEV = 2


def unit_rows(x):
    x = x.astype(jnp.float32)
    return x * lax.rsqrt(jnp.sum(x * x, axis=-1, keepdims=True) + 1e-06)


def unit_lower_inverse(lower):
    highest = lax.Precision.HIGHEST
    n = lower.shape[-1]
    rows = jnp.arange(n)[:, None]
    cols = jnp.arange(n)[None, :]
    inv = None
    b = 1
    while b < n:
        sel = (rows // (2 * b) == cols // (2 * b)) & ((rows // b) % 2 == 1) & ((cols // b) % 2 == 0)
        c = jnp.where(sel, lower, 0.0)
        if inv is None:
            inv = lax.optimization_barrier(jnp.eye(n, dtype=lower.dtype) - c)
        else:
            mc = jnp.einsum("...ij,...jk->...ik", inv, c, precision=highest)
            inv = inv - jnp.einsum("...ij,...jk->...ik", mc, inv, precision=highest)
        b *= 2
    return inv


def run_experts(arrived, expert_gate_up, expert_down):
    provider_rows, count, part, width = arrived.shape
    rows = arrived.transpose(1, 0, 2, 3).reshape(count, provider_rows * part, width)
    both = jnp.einsum("erd,edf->erf", rows, expert_gate_up, preferred_element_type=jnp.float32)
    inner = (jax.nn.silu(both[..., :FFE]) * both[..., FFE:]).astype(jnp.bfloat16)
    result = jnp.einsum(
        "erf,efd->erd", inner, expert_down, preferred_element_type=jnp.float32
    ).astype(jnp.bfloat16)
    return result.reshape(count, provider_rows, part, width).transpose(1, 0, 2, 3)


def shards(
    queries,
    keys,
    values,
    gate_input,
    beta,
    log_decay,
    norm_gain,
    w_out,
    hidden,
    post_gain,
    routes,
    route_scores,
    expert_gate_up,
    expert_down,
    accepted,
):
    highest = lax.Precision.HIGHEST
    seq = queries.shape[1]
    n_ctx = lax.axis_size("ctx")
    n_req = lax.axis_size("req")
    n_dev = n_ctx * n_req
    experts = EXP_DEV * n_dev
    cap = max(2, 3 * seq * TOPK // (2 * experts))
    kh_dev = HK // n_ctx
    hv_dev = HV // n_ctx
    qw = kh_dev * DK
    vw = hv_dev * DV

    rates_decay = (
        jnp.stack([beta[0], log_decay[0]]).reshape(2, n_ctx, hv_dev, seq).transpose(1, 0, 2, 3)
    )
    hi = lax.reduce_precision(rates_decay, exponent_bits=8, mantissa_bits=7)
    rest = rates_decay - hi
    mid = lax.reduce_precision(rest, exponent_bits=8, mantissa_bits=7)
    lo = lax.reduce_precision(rest - mid, exponent_bits=8, mantissa_bits=7)
    width = 2 * qw + vw
    parts = jnp.stack([hi, mid, lo], axis=1).astype(jnp.bfloat16).reshape(n_ctx, -1)
    extra = -(-parts.shape[-1] // width)
    parts = jnp.pad(parts, ((0, 0), (0, extra * width - parts.shape[-1]))).reshape(n_ctx, extra, width)
    packed = jnp.concatenate(
        [
            jnp.concatenate(
                [
                    queries[0].reshape(seq, n_ctx, qw),
                    keys[0].reshape(seq, n_ctx, qw),
                    values[0].reshape(seq, n_ctx, vw),
                ],
                axis=2,
            ).transpose(1, 0, 2),
            parts,
        ],
        axis=1,
    )
    got = lax.all_to_all(packed, "ctx", 0, 0, tiled=True)
    arrived = got[:, :seq]
    rd = (
        got[:, seq:]
        .reshape(n_ctx, -1)[:, : 3 * 2 * hv_dev * seq]
        .astype(jnp.float32)
        .reshape(n_ctx, 3, 2, hv_dev, seq)
    )
    rd = (rd[:, 0] + rd[:, 1]) + rd[:, 2]
    rates = rd[:, 0].transpose(1, 0, 2)
    gamma = jnp.cumsum(rd[:, 1].transpose(1, 0, 2), axis=-1)
    qc = unit_rows(arrived[..., :qw]) * DK ** (-0.5)
    kc = unit_rows(arrived[..., qw : 2 * qw])
    vc = (
        arrived[..., 2 * qw : 2 * qw + vw]
        .astype(jnp.float32)
        .reshape(n_ctx, seq, hv_dev, DV)
        .transpose(2, 0, 1, 3)
    )

    ordinals = jnp.arange(seq)
    before = ordinals[:, None] > ordinals[None, :]
    upto = ordinals[:, None] >= ordinals[None, :]
    spans = gamma[..., :, None] - gamma[..., None, :]
    pair_decay = jnp.exp(jnp.where(upto, spans, 0.0))
    key_key = jnp.einsum("ntd,nsd->nts", kc, kc, precision=highest)
    lower = jnp.where(before, pair_decay * key_key[None] * rates[..., None, :], 0.0)
    inverse = unit_lower_inverse(lower)
    growth = jnp.exp(gamma)
    right = jnp.concatenate(
        [vc, growth[..., None] * jnp.broadcast_to(kc[None], vc.shape)], axis=-1
    )
    solved = jnp.einsum("hnts,hnsf->hntf", inverse, right, precision=highest)
    solved_values = solved[..., :DV]
    solved_keys = solved[..., DV:]
    tail = rates * jnp.exp(gamma[..., -1:] - gamma)
    weighted = (kc[None] * tail[..., None]).reshape(hv_dev * n_ctx, seq, DK)
    carried = jnp.einsum(
        "btd,btf->bdf", weighted, solved.reshape(hv_dev * n_ctx, seq, DV + DK), precision=highest
    ).reshape(hv_dev, n_ctx, DK, DV + DK)
    growth_last = growth[..., -1]
    key_part = carried[..., DV:]
    offset = carried[..., :DV]
    state = offset[:, 0]
    states = [jnp.zeros_like(state), state]
    for n in range(1, n_ctx - 1):
        state = (
            offset[:, n]
            + growth_last[:, n, None, None] * state
            - jnp.einsum("hde,hef->hdf", key_part[:, n], state, precision=highest)
        )
        states.append(state)
    states = jnp.stack(states, axis=1)
    pseudo = solved_values - jnp.einsum("hntd,hnde->hnte", solved_keys, states, precision=highest)
    query_key = jnp.einsum("ntd,nsd->nts", qc, kc, precision=highest)
    mixing = jnp.where(upto, pair_decay * query_key[None] * rates[..., None, :], 0.0)
    core = growth[..., None] * jnp.einsum("ntd,hnde->hnte", qc, states, precision=highest)
    core = core + jnp.einsum("hnts,hnse->hnte", mixing, pseudo, precision=highest)

    last = accepted[0] - 1
    chunk = last // seq
    local = last % seq
    gamma_chunk = lax.dynamic_index_in_dim(gamma, chunk, axis=1, keepdims=False)
    rates_chunk = lax.dynamic_index_in_dim(rates, chunk, axis=1, keepdims=False)
    pseudo_chunk = lax.dynamic_index_in_dim(pseudo, chunk, axis=1, keepdims=False)
    state_chunk = lax.dynamic_index_in_dim(states, chunk, axis=1, keepdims=False)
    keys_chunk = lax.dynamic_index_in_dim(kc, chunk, axis=0, keepdims=False)
    gamma_at = lax.dynamic_index_in_dim(gamma_chunk, local, axis=1, keepdims=False)
    keep = jnp.where(
        ordinals[None, :] <= local,
        rates_chunk * jnp.exp(jnp.minimum(gamma_at[:, None] - gamma_chunk, 0.0)),
        0.0,
    )
    final_state = jnp.exp(gamma_at)[:, None, None] * state_chunk + jnp.einsum(
        "td,hte->hde", keys_chunk, keep[..., None] * pseudo_chunk, precision=highest
    )
    final_state = final_state[None]

    scale = lax.rsqrt(jnp.mean(core * core, axis=-1, keepdims=True) + 1e-06)
    shaped = (core * scale * norm_gain).astype(jnp.bfloat16)
    shaped = shaped.transpose(1, 2, 0, 3).reshape(n_ctx, seq, vw)
    back = lax.all_to_all(shaped, "ctx", 0, 0, tiled=True)
    gating = jax.nn.silu(gate_input[0].astype(jnp.float32).reshape(seq, n_ctx, vw).transpose(1, 0, 2))
    normed = (back.astype(jnp.float32) * gating).astype(jnp.bfloat16)
    resid = hidden[0].astype(jnp.float32) + jnp.einsum(
        "jtf,jfd->td",
        normed,
        w_out.reshape(n_ctx, vw, D),
        preferred_element_type=jnp.float32,
    )
    moe_in = (
        resid * lax.rsqrt(jnp.mean(resid * resid, axis=-1, keepdims=True) + 1e-06) * post_gain
    ).astype(jnp.bfloat16)

    flat_ids = routes[0].reshape(-1)
    onehot = (flat_ids[:, None] == jnp.arange(experts, dtype=jnp.int32)[None, :]).astype(jnp.int32)
    earlier = jnp.cumsum(onehot, axis=0) - onehot
    slot = jnp.sum(earlier * onehot, axis=1)
    target = (flat_ids * cap + slot).reshape(seq, TOPK)
    slots = (
        jnp.arange(experts * cap, dtype=jnp.int32)
        .reshape(n_dev, EXP_DEV, cap)
        .transpose(0, 2, 1)
    )
    hits = target[None, None, None, :, :] == slots[..., None, None]
    dispatch = jnp.sum(jnp.where(hits, 1.0, 0.0), axis=-1).astype(jnp.bfloat16)
    outgoing_rows = jnp.einsum(
        "dcet,tf->dcef", dispatch, moe_in, preferred_element_type=jnp.float32
    ).astype(jnp.bfloat16)
    arrived_rows = lax.all_to_all(
        outgoing_rows, ("ctx", "req"), split_axis=0, concat_axis=0, tiled=True
    )
    both = jnp.einsum(
        "scex,exf->escf", arrived_rows, expert_gate_up, preferred_element_type=jnp.float32
    )
    inner = (jax.nn.silu(both[..., :FFE]) * both[..., FFE:]).astype(jnp.bfloat16)
    result = jnp.einsum(
        "escf,efx->scex", inner, expert_down, preferred_element_type=jnp.float32
    ).astype(jnp.bfloat16)
    returned = lax.all_to_all(result, ("ctx", "req"), split_axis=0, concat_axis=0, tiled=True)
    scores = route_scores[0]
    mix_weights = scores / jnp.sum(scores, axis=-1, keepdims=True)
    combine = jnp.sum(jnp.where(hits, mix_weights, 0.0), axis=-1)
    combine_hi = lax.reduce_precision(combine, exponent_bits=8, mantissa_bits=7)
    combine_lo = combine - combine_hi
    halves = jnp.concatenate([combine_hi, combine_lo], axis=-1).astype(jnp.bfloat16)
    both_out = jnp.einsum(
        "dcet,dcex->tx", halves, returned, preferred_element_type=jnp.float32
    )
    moe_out = both_out[:seq] + both_out[seq:]
    layer_out = (resid + moe_out).astype(jnp.bfloat16)[None]
    return (layer_out, final_state)


def solution(mesh):
    placed = (
        P("req", "ctx", None),
        P("req", "ctx", None),
        P("req", "ctx", None),
        P("req", "ctx", None),
        P("req", None, "ctx"),
        P("req", None, "ctx"),
        P(),
        P(),
        P("req", "ctx", None),
        P(),
        P("req", "ctx", None),
        P("req", "ctx", None),
        P(("ctx", "req"), None, None),
        P(("ctx", "req"), None, None),
        P("req"),
    )
    return jax.shard_map(
        shards,
        mesh=mesh,
        in_specs=placed,
        out_specs=(P("req", "ctx", None), P("req", "ctx", None, None)),
        check_vma=False,
    )
```

```python
import jax
import jax.numpy as jnp
from jax import lax
from jax.sharding import PartitionSpec as P

D = 2048
HK = 8
HV = 16
DK = 128
DV = 128
FFE = 512
TOPK = 10
EXP_DEV = 2


def unit_rows(x):
    x = x.astype(jnp.float32)
    return x * lax.rsqrt(jnp.sum(x * x, axis=-1, keepdims=True) + 1e-06)


def unit_lower_inverse(lower):
    highest = lax.Precision.HIGHEST
    n = lower.shape[-1]
    rows = jnp.arange(n)[:, None]
    cols = jnp.arange(n)[None, :]
    first = (rows // 2 == cols // 2) & (rows % 2 == 1) & (cols % 2 == 0)
    inv = lax.optimization_barrier(jnp.eye(n, dtype=lower.dtype) - jnp.where(first, lower, 0.0))

    def level(i, inv):
        b = jnp.left_shift(jnp.int32(1), i)
        sel = (rows // (2 * b) == cols // (2 * b)) & ((rows // b) % 2 == 1) & ((cols // b) % 2 == 0)
        c = jnp.where(sel, lower, 0.0)
        mc = jnp.einsum("...ij,...jk->...ik", inv, c, precision=highest)
        return inv - jnp.einsum("...ij,...jk->...ik", mc, inv, precision=highest)

    inv = lax.fori_loop(1, n.bit_length() - 1, level, inv)
    return inv


def run_experts(arrived, expert_gate_up, expert_down):
    provider_rows, count, part, width = arrived.shape
    rows = arrived.transpose(1, 0, 2, 3).reshape(count, provider_rows * part, width)
    both = jnp.einsum("erd,edf->erf", rows, expert_gate_up, preferred_element_type=jnp.float32)
    inner = (jax.nn.silu(both[..., :FFE]) * both[..., FFE:]).astype(jnp.bfloat16)
    result = jnp.einsum(
        "erf,efd->erd", inner, expert_down, preferred_element_type=jnp.float32
    ).astype(jnp.bfloat16)
    return result.reshape(count, provider_rows, part, width).transpose(1, 0, 2, 3)


def shards(
    queries,
    keys,
    values,
    gate_input,
    beta,
    log_decay,
    norm_gain,
    w_out,
    hidden,
    post_gain,
    routes,
    route_scores,
    expert_gate_up,
    expert_down,
    accepted,
):
    highest = lax.Precision.HIGHEST
    seq = queries.shape[1]
    n_ctx = lax.axis_size("ctx")
    n_req = lax.axis_size("req")
    n_dev = n_ctx * n_req
    experts = EXP_DEV * n_dev
    cap = max(2, 3 * seq * TOPK // (2 * experts))
    kh_dev = HK // n_ctx
    hv_dev = HV // n_ctx
    qw = kh_dev * DK
    vw = hv_dev * DV

    rates_decay = (
        jnp.stack([beta[0], log_decay[0]]).reshape(2, n_ctx, hv_dev, seq).transpose(1, 0, 2, 3)
    )
    hi = lax.reduce_precision(rates_decay, exponent_bits=8, mantissa_bits=7)
    rest = rates_decay - hi
    mid = lax.reduce_precision(rest, exponent_bits=8, mantissa_bits=7)
    lo = lax.reduce_precision(rest - mid, exponent_bits=8, mantissa_bits=7)
    width = 2 * qw + vw
    parts = jnp.stack([hi, mid, lo], axis=1).astype(jnp.bfloat16).reshape(n_ctx, -1)
    extra = -(-parts.shape[-1] // width)
    parts = jnp.pad(parts, ((0, 0), (0, extra * width - parts.shape[-1]))).reshape(n_ctx, extra, width)
    packed = jnp.concatenate(
        [
            jnp.concatenate(
                [
                    queries[0].reshape(seq, n_ctx, qw),
                    keys[0].reshape(seq, n_ctx, qw),
                    values[0].reshape(seq, n_ctx, vw),
                ],
                axis=2,
            ).transpose(1, 0, 2),
            parts,
        ],
        axis=1,
    )
    got = lax.all_to_all(packed, "ctx", 0, 0, tiled=True)
    arrived = got[:, :seq]
    rd = (
        got[:, seq:]
        .reshape(n_ctx, -1)[:, : 3 * 2 * hv_dev * seq]
        .astype(jnp.float32)
        .reshape(n_ctx, 3, 2, hv_dev, seq)
    )
    rd = (rd[:, 0] + rd[:, 1]) + rd[:, 2]
    rates = rd[:, 0].transpose(1, 0, 2)
    gamma = jnp.cumsum(rd[:, 1].transpose(1, 0, 2), axis=-1)
    qc = unit_rows(arrived[..., :qw]) * DK ** (-0.5)
    kc = unit_rows(arrived[..., qw : 2 * qw])
    vc = (
        arrived[..., 2 * qw : 2 * qw + vw]
        .astype(jnp.float32)
        .reshape(n_ctx, seq, hv_dev, DV)
        .transpose(2, 0, 1, 3)
    )

    ordinals = jnp.arange(seq)
    before = ordinals[:, None] > ordinals[None, :]
    upto = ordinals[:, None] >= ordinals[None, :]
    spans = gamma[..., :, None] - gamma[..., None, :]
    pair_decay = jnp.exp(jnp.where(upto, spans, 0.0))
    key_key = jnp.einsum("ntd,nsd->nts", kc, kc, precision=highest)
    lower = jnp.where(before, pair_decay * key_key[None] * rates[..., None, :], 0.0)
    inverse = unit_lower_inverse(lower)
    growth = jnp.exp(gamma)
    right = jnp.concatenate(
        [vc, growth[..., None] * jnp.broadcast_to(kc[None], vc.shape)], axis=-1
    )
    solved = jnp.einsum("hnts,hnsf->hntf", inverse, right, precision=highest)
    solved_values = solved[..., :DV]
    solved_keys = solved[..., DV:]
    tail = rates * jnp.exp(gamma[..., -1:] - gamma)
    weighted = (kc[None] * tail[..., None]).reshape(hv_dev * n_ctx, seq, DK)
    carried = jnp.einsum(
        "btd,btf->bdf", weighted, solved.reshape(hv_dev * n_ctx, seq, DV + DK), precision=highest
    ).reshape(hv_dev, n_ctx, DK, DV + DK)
    growth_last = growth[..., -1]
    key_part = carried[..., DV:]
    offset = carried[..., :DV]
    state = offset[:, 0]
    states = [jnp.zeros_like(state), state]
    for n in range(1, n_ctx - 1):
        state = (
            offset[:, n]
            + growth_last[:, n, None, None] * state
            - jnp.einsum("hde,hef->hdf", key_part[:, n], state, precision=highest)
        )
        states.append(state)
    states = jnp.stack(states, axis=1)
    pseudo = solved_values - jnp.einsum("hntd,hnde->hnte", solved_keys, states, precision=highest)
    query_key = jnp.einsum("ntd,nsd->nts", qc, kc, precision=highest)
    mixing = jnp.where(upto, pair_decay * query_key[None] * rates[..., None, :], 0.0)
    core = growth[..., None] * jnp.einsum("ntd,hnde->hnte", qc, states, precision=highest)
    core = core + jnp.einsum("hnts,hnse->hnte", mixing, pseudo, precision=highest)

    last = accepted[0] - 1
    chunk = last // seq
    local = last % seq
    gamma_chunk = lax.dynamic_index_in_dim(gamma, chunk, axis=1, keepdims=False)
    rates_chunk = lax.dynamic_index_in_dim(rates, chunk, axis=1, keepdims=False)
    pseudo_chunk = lax.dynamic_index_in_dim(pseudo, chunk, axis=1, keepdims=False)
    state_chunk = lax.dynamic_index_in_dim(states, chunk, axis=1, keepdims=False)
    keys_chunk = lax.dynamic_index_in_dim(kc, chunk, axis=0, keepdims=False)
    gamma_at = lax.dynamic_index_in_dim(gamma_chunk, local, axis=1, keepdims=False)
    keep = jnp.where(
        ordinals[None, :] <= local,
        rates_chunk * jnp.exp(jnp.minimum(gamma_at[:, None] - gamma_chunk, 0.0)),
        0.0,
    )
    final_state = jnp.exp(gamma_at)[:, None, None] * state_chunk + jnp.einsum(
        "td,hte->hde", keys_chunk, keep[..., None] * pseudo_chunk, precision=highest
    )
    final_state = final_state[None]

    scale = lax.rsqrt(jnp.mean(core * core, axis=-1, keepdims=True) + 1e-06)
    shaped = (core * scale * norm_gain).astype(jnp.bfloat16)
    shaped = shaped.transpose(1, 2, 0, 3).reshape(n_ctx, seq, vw)
    back = lax.all_to_all(shaped, "ctx", 0, 0, tiled=True)
    gating = jax.nn.silu(gate_input[0].astype(jnp.float32).reshape(seq, n_ctx, vw).transpose(1, 0, 2))
    normed = (back.astype(jnp.float32) * gating).astype(jnp.bfloat16)
    resid = hidden[0].astype(jnp.float32) + jnp.einsum(
        "jtf,jfd->td",
        normed,
        w_out.reshape(n_ctx, vw, D),
        preferred_element_type=jnp.float32,
    )
    moe_in = (
        resid * lax.rsqrt(jnp.mean(resid * resid, axis=-1, keepdims=True) + 1e-06) * post_gain
    ).astype(jnp.bfloat16)

    flat_ids = routes[0].reshape(-1)
    onehot = (flat_ids[:, None] == jnp.arange(experts, dtype=jnp.int32)[None, :]).astype(jnp.int32)
    earlier = jnp.cumsum(onehot, axis=0) - onehot
    slot = jnp.sum(earlier * onehot, axis=1)
    target = (flat_ids * cap + slot).reshape(seq, TOPK)
    slots = (
        jnp.arange(experts * cap, dtype=jnp.int32)
        .reshape(n_dev, EXP_DEV, cap)
        .transpose(0, 2, 1)
    )
    hits = target[None, None, None, :, :] == slots[..., None, None]
    dispatch = jnp.sum(jnp.where(hits, 1.0, 0.0), axis=-1).astype(jnp.bfloat16)
    outgoing_rows = jnp.einsum(
        "dcet,tf->dcef", dispatch, moe_in, preferred_element_type=jnp.float32
    ).astype(jnp.bfloat16)
    arrived_rows = lax.all_to_all(
        outgoing_rows, ("ctx", "req"), split_axis=0, concat_axis=0, tiled=True
    )
    both = jnp.einsum(
        "scex,exf->escf", arrived_rows, expert_gate_up, preferred_element_type=jnp.float32
    )
    inner = (jax.nn.silu(both[..., :FFE]) * both[..., FFE:]).astype(jnp.bfloat16)
    result = jnp.einsum(
        "escf,efx->scex", inner, expert_down, preferred_element_type=jnp.float32
    ).astype(jnp.bfloat16)
    returned = lax.all_to_all(result, ("ctx", "req"), split_axis=0, concat_axis=0, tiled=True)
    scores = route_scores[0]
    mix_weights = scores / jnp.sum(scores, axis=-1, keepdims=True)
    combine = jnp.sum(jnp.where(hits, mix_weights, 0.0), axis=-1)
    combine_hi = lax.reduce_precision(combine, exponent_bits=8, mantissa_bits=7)
    combine_lo = combine - combine_hi
    halves = jnp.concatenate([combine_hi, combine_lo], axis=-1).astype(jnp.bfloat16)
    both_out = jnp.einsum(
        "dcet,dcex->tx", halves, returned, preferred_element_type=jnp.float32
    )
    moe_out = both_out[:seq] + both_out[seq:]
    layer_out = (resid + moe_out).astype(jnp.bfloat16)[None]
    return (layer_out, final_state)


def solution(mesh):
    placed = (
        P("req", "ctx", None),
        P("req", "ctx", None),
        P("req", "ctx", None),
        P("req", "ctx", None),
        P("req", None, "ctx"),
        P("req", None, "ctx"),
        P(),
        P(),
        P("req", "ctx", None),
        P(),
        P("req", "ctx", None),
        P("req", "ctx", None),
        P(("ctx", "req"), None, None),
        P(("ctx", "req"), None, None),
        P("req"),
    )
    return jax.shard_map(
        shards,
        mesh=mesh,
        in_specs=placed,
        out_specs=(P("req", "ctx", None), P("req", "ctx", None, None)),
        check_vma=False,
    )
```

```python
import jax
import jax.numpy as jnp
from jax import lax
from jax.sharding import PartitionSpec as P

D = 2048
HK = 8
HV = 16
DK = 128
DV = 128
FFE = 512
TOPK = 10
EXP_DEV = 2


def unit_rows(x):
    x = x.astype(jnp.float32)
    return x * lax.rsqrt(jnp.sum(x * x, axis=-1, keepdims=True) + 1e-06)


def unit_lower_inverse(lower):
    highest = lax.Precision.HIGHEST
    n = lower.shape[-1]
    rows = jnp.arange(n)[:, None]
    cols = jnp.arange(n)[None, :]
    first = (rows // 2 == cols // 2) & (rows % 2 == 1) & (cols % 2 == 0)
    inv = lax.optimization_barrier(jnp.eye(n, dtype=lower.dtype) - jnp.where(first, lower, 0.0))

    def level(i, inv):
        b = jnp.left_shift(jnp.int32(1), i)
        sel = (rows // (2 * b) == cols // (2 * b)) & ((rows // b) % 2 == 1) & ((cols // b) % 2 == 0)
        c = jnp.where(sel, lower, 0.0)
        mc = jnp.einsum("...ij,...jk->...ik", inv, c, precision=highest)
        return inv - jnp.einsum("...ij,...jk->...ik", mc, inv, precision=highest)

    inv = lax.fori_loop(1, n.bit_length() - 1, level, inv)
    return inv


def run_experts(arrived, expert_gate_up, expert_down):
    provider_rows, count, part, width = arrived.shape
    rows = arrived.transpose(1, 0, 2, 3).reshape(count, provider_rows * part, width)
    both = jnp.einsum("erd,edf->erf", rows, expert_gate_up, preferred_element_type=jnp.float32)
    inner = (jax.nn.silu(both[..., :FFE]) * both[..., FFE:]).astype(jnp.bfloat16)
    result = jnp.einsum(
        "erf,efd->erd", inner, expert_down, preferred_element_type=jnp.float32
    ).astype(jnp.bfloat16)
    return result.reshape(count, provider_rows, part, width).transpose(1, 0, 2, 3)


def shards(
    queries,
    keys,
    values,
    gate_input,
    beta,
    log_decay,
    norm_gain,
    w_out,
    hidden,
    post_gain,
    routes,
    route_scores,
    expert_gate_up,
    expert_down,
    accepted,
):
    highest = lax.Precision.HIGHEST
    seq = queries.shape[1]
    n_ctx = lax.axis_size("ctx")
    n_req = lax.axis_size("req")
    n_dev = n_ctx * n_req
    experts = EXP_DEV * n_dev
    cap = max(2, 3 * seq * TOPK // (2 * experts))
    kh_dev = HK // n_ctx
    hv_dev = HV // n_ctx
    qw = kh_dev * DK
    vw = hv_dev * DV

    rates_decay = (
        jnp.stack([beta[0], log_decay[0]]).reshape(2, n_ctx, hv_dev, seq).transpose(1, 0, 2, 3)
    )
    hi = lax.reduce_precision(rates_decay, exponent_bits=8, mantissa_bits=7)
    rest = rates_decay - hi
    mid = lax.reduce_precision(rest, exponent_bits=8, mantissa_bits=7)
    lo = lax.reduce_precision(rest - mid, exponent_bits=8, mantissa_bits=7)
    width = 2 * qw + vw
    parts = jnp.stack([hi, mid, lo], axis=1).astype(jnp.bfloat16).reshape(n_ctx, -1)
    extra = -(-parts.shape[-1] // width)
    parts = jnp.pad(parts, ((0, 0), (0, extra * width - parts.shape[-1]))).reshape(n_ctx, extra, width)
    packed = jnp.concatenate(
        [
            jnp.concatenate(
                [
                    queries[0].reshape(seq, n_ctx, qw),
                    keys[0].reshape(seq, n_ctx, qw),
                    values[0].reshape(seq, n_ctx, vw),
                ],
                axis=2,
            ).transpose(1, 0, 2),
            parts,
        ],
        axis=1,
    )
    got = lax.all_to_all(packed, "ctx", 0, 0, tiled=True)
    arrived = got[:, :seq]
    rd = (
        got[:, seq:]
        .reshape(n_ctx, -1)[:, : 3 * 2 * hv_dev * seq]
        .astype(jnp.float32)
        .reshape(n_ctx, 3, 2, hv_dev, seq)
    )
    rd = (rd[:, 0] + rd[:, 1]) + rd[:, 2]
    rates = rd[:, 0].transpose(1, 0, 2)
    gamma = jnp.cumsum(rd[:, 1].transpose(1, 0, 2), axis=-1)
    qc = unit_rows(arrived[..., :qw]) * DK ** (-0.5)
    kc = unit_rows(arrived[..., qw : 2 * qw])
    vc = (
        arrived[..., 2 * qw : 2 * qw + vw]
        .astype(jnp.float32)
        .reshape(n_ctx, seq, hv_dev, DV)
        .transpose(2, 0, 1, 3)
    )

    ordinals = jnp.arange(seq)
    before = ordinals[:, None] > ordinals[None, :]
    upto = ordinals[:, None] >= ordinals[None, :]
    spans = gamma[..., :, None] - gamma[..., None, :]
    pair_decay = jnp.exp(jnp.where(upto, spans, 0.0))
    key_key = jnp.einsum("ntd,nsd->nts", kc, kc, precision=highest)
    lower = jnp.where(before, pair_decay * key_key[None] * rates[..., None, :], 0.0)
    inverse = unit_lower_inverse(lower)
    growth = jnp.exp(gamma)
    right = jnp.concatenate(
        [vc, growth[..., None] * jnp.broadcast_to(kc[None], vc.shape)], axis=-1
    )
    solved = jnp.einsum("hnts,hnsf->hntf", inverse, right, precision=highest)
    solved_values = solved[..., :DV]
    solved_keys = solved[..., DV:]
    tail = rates * jnp.exp(gamma[..., -1:] - gamma)
    weighted = (kc[None] * tail[..., None]).reshape(hv_dev * n_ctx, seq, DK)
    carried = jnp.einsum(
        "btd,btf->bdf", weighted, solved.reshape(hv_dev * n_ctx, seq, DV + DK), precision=highest
    ).reshape(hv_dev, n_ctx, DK, DV + DK)
    growth_last = growth[..., -1]
    key_part = carried[..., DV:]
    offset = carried[..., :DV]
    state = offset[:, 0]
    states = [jnp.zeros_like(state), state]
    for n in range(1, n_ctx - 1):
        state = (
            offset[:, n]
            + growth_last[:, n, None, None] * state
            - jnp.einsum("hde,hef->hdf", key_part[:, n], state, precision=highest)
        )
        states.append(state)
    states = jnp.stack(states, axis=1)
    pseudo = solved_values - jnp.einsum("hntd,hnde->hnte", solved_keys, states, precision=highest)
    query_key = jnp.einsum("ntd,nsd->nts", qc, kc, precision=highest)
    mixing = jnp.where(upto, pair_decay * query_key[None] * rates[..., None, :], 0.0)
    core = growth[..., None] * jnp.einsum("ntd,hnde->hnte", qc, states, precision=highest)
    core = core + jnp.einsum("hnts,hnse->hnte", mixing, pseudo, precision=highest)

    last = accepted[0] - 1
    chunk = last // seq
    local = last % seq
    gamma_chunk = lax.dynamic_index_in_dim(gamma, chunk, axis=1, keepdims=False)
    rates_chunk = lax.dynamic_index_in_dim(rates, chunk, axis=1, keepdims=False)
    pseudo_chunk = lax.dynamic_index_in_dim(pseudo, chunk, axis=1, keepdims=False)
    state_chunk = lax.dynamic_index_in_dim(states, chunk, axis=1, keepdims=False)
    keys_chunk = lax.dynamic_index_in_dim(kc, chunk, axis=0, keepdims=False)
    gamma_at = lax.dynamic_index_in_dim(gamma_chunk, local, axis=1, keepdims=False)
    keep = jnp.where(
        ordinals[None, :] <= local,
        rates_chunk * jnp.exp(jnp.minimum(gamma_at[:, None] - gamma_chunk, 0.0)),
        0.0,
    )
    final_state = jnp.exp(gamma_at)[:, None, None] * state_chunk + jnp.einsum(
        "td,hte->hde", keys_chunk, keep[..., None] * pseudo_chunk, precision=highest
    )
    final_state = final_state[None]

    scale = lax.rsqrt(jnp.mean(core * core, axis=-1, keepdims=True) + 1e-06)
    shaped = (core * scale * norm_gain).astype(jnp.bfloat16)
    shaped = shaped.transpose(1, 2, 0, 3).reshape(n_ctx, seq, vw)
    back = lax.all_to_all(shaped, "ctx", 0, 0, tiled=True)
    gating = jax.nn.silu(gate_input[0].astype(jnp.float32).reshape(seq, n_ctx, vw).transpose(1, 0, 2))
    normed = (back.astype(jnp.float32) * gating).astype(jnp.bfloat16)
    normed = normed.transpose(1, 0, 2).reshape(seq, HV * DV)
    resid = hidden[0].astype(jnp.float32) + jnp.dot(
        normed, w_out, preferred_element_type=jnp.float32
    )
    moe_in = (
        resid * lax.rsqrt(jnp.mean(resid * resid, axis=-1, keepdims=True) + 1e-06) * post_gain
    ).astype(jnp.bfloat16)

    flat_ids = routes[0].reshape(-1)
    onehot = (flat_ids[:, None] == jnp.arange(experts, dtype=jnp.int32)[None, :]).astype(jnp.int32)
    earlier = jnp.cumsum(onehot, axis=0) - onehot
    slot = jnp.sum(earlier * onehot, axis=1)
    target = (flat_ids * cap + slot).reshape(seq, TOPK)
    slots = (
        jnp.arange(experts * cap, dtype=jnp.int32)
        .reshape(n_dev, EXP_DEV, cap)
        .transpose(0, 2, 1)
    )
    hits = target[None, None, None, :, :] == slots[..., None, None]
    dispatch = jnp.sum(jnp.where(hits, 1.0, 0.0), axis=-1).astype(jnp.bfloat16)
    outgoing_rows = jnp.einsum(
        "dcet,tf->dcef", dispatch, moe_in, preferred_element_type=jnp.float32
    ).astype(jnp.bfloat16)
    arrived_rows = lax.all_to_all(
        outgoing_rows, ("ctx", "req"), split_axis=0, concat_axis=0, tiled=True
    )
    both = jnp.einsum(
        "scex,exf->escf", arrived_rows, expert_gate_up, preferred_element_type=jnp.float32
    )
    inner = (jax.nn.silu(both[..., :FFE]) * both[..., FFE:]).astype(jnp.bfloat16)
    result = jnp.einsum(
        "escf,efx->scex", inner, expert_down, preferred_element_type=jnp.float32
    ).astype(jnp.bfloat16)
    returned = lax.all_to_all(result, ("ctx", "req"), split_axis=0, concat_axis=0, tiled=True)
    scores = route_scores[0]
    mix_weights = scores / jnp.sum(scores, axis=-1, keepdims=True)
    combine = jnp.sum(jnp.where(hits, mix_weights, 0.0), axis=-1)
    combine_hi = lax.reduce_precision(combine, exponent_bits=8, mantissa_bits=7)
    combine_lo = combine - combine_hi
    halves = jnp.concatenate([combine_hi, combine_lo], axis=-1).astype(jnp.bfloat16)
    both_out = jnp.einsum(
        "dcet,dcex->tx", halves, returned, preferred_element_type=jnp.float32
    )
    moe_out = both_out[:seq] + both_out[seq:]
    layer_out = (resid + moe_out).astype(jnp.bfloat16)[None]
    return (layer_out, final_state)


def solution(mesh):
    placed = (
        P("req", "ctx", None),
        P("req", "ctx", None),
        P("req", "ctx", None),
        P("req", "ctx", None),
        P("req", None, "ctx"),
        P("req", None, "ctx"),
        P(),
        P(),
        P("req", "ctx", None),
        P(),
        P("req", "ctx", None),
        P("req", "ctx", None),
        P(("ctx", "req"), None, None),
        P(("ctx", "req"), None, None),
        P("req"),
    )
    return jax.shard_map(
        shards,
        mesh=mesh,
        in_specs=placed,
        out_specs=(P("req", "ctx", None), P("req", "ctx", None, None)),
        check_vma=False,
    )
```

```python
import jax
import jax.numpy as jnp
from jax import lax
from jax.sharding import PartitionSpec as P

D = 2048
HK = 8
HV = 16
DK = 128
DV = 128
FFE = 512
TOPK = 10
EXP_DEV = 2


def unit_rows(x):
    x = x.astype(jnp.float32)
    return x * lax.rsqrt(jnp.sum(x * x, axis=-1, keepdims=True) + 1e-06)


def unit_lower_inverse(lower):
    highest = lax.Precision.HIGHEST
    n = lower.shape[-1]
    rows = jnp.arange(n)[:, None]
    cols = jnp.arange(n)[None, :]
    first = (rows // 2 == cols // 2) & (rows % 2 == 1) & (cols % 2 == 0)
    inv = lax.optimization_barrier(jnp.eye(n, dtype=lower.dtype) - jnp.where(first, lower, 0.0))

    def level(i, inv):
        b = jnp.left_shift(jnp.int32(1), i)
        sel = (rows // (2 * b) == cols // (2 * b)) & ((rows // b) % 2 == 1) & ((cols // b) % 2 == 0)
        c = jnp.where(sel, lower, 0.0)
        mc = jnp.einsum("...ij,...jk->...ik", inv, c, precision=highest)
        return inv - jnp.einsum("...ij,...jk->...ik", mc, inv, precision=highest)

    inv = lax.fori_loop(1, n.bit_length() - 1, level, inv)
    return inv


def run_experts(arrived, expert_gate_up, expert_down):
    provider_rows, count, part, width = arrived.shape
    rows = arrived.transpose(1, 0, 2, 3).reshape(count, provider_rows * part, width)
    both = jnp.einsum("erd,edf->erf", rows, expert_gate_up, preferred_element_type=jnp.float32)
    inner = (jax.nn.silu(both[..., :FFE]) * both[..., FFE:]).astype(jnp.bfloat16)
    result = jnp.einsum(
        "erf,efd->erd", inner, expert_down, preferred_element_type=jnp.float32
    ).astype(jnp.bfloat16)
    return result.reshape(count, provider_rows, part, width).transpose(1, 0, 2, 3)


def shards(
    queries,
    keys,
    values,
    gate_input,
    beta,
    log_decay,
    norm_gain,
    w_out,
    hidden,
    post_gain,
    routes,
    route_scores,
    expert_gate_up,
    expert_down,
    accepted,
):
    highest = lax.Precision.HIGHEST
    seq = queries.shape[1]
    n_ctx = lax.axis_size("ctx")
    n_req = lax.axis_size("req")
    n_dev = n_ctx * n_req
    experts = EXP_DEV * n_dev
    cap = max(2, 3 * seq * TOPK // (2 * experts))
    kh_dev = HK // n_ctx
    hv_dev = HV // n_ctx
    qw = kh_dev * DK
    vw = hv_dev * DV

    rates_decay = (
        jnp.stack([beta[0], log_decay[0]]).reshape(2, n_ctx, hv_dev, seq).transpose(1, 0, 2, 3)
    )
    hi = lax.reduce_precision(rates_decay, exponent_bits=8, mantissa_bits=7)
    rest = rates_decay - hi
    mid = lax.reduce_precision(rest, exponent_bits=8, mantissa_bits=7)
    lo = lax.reduce_precision(rest - mid, exponent_bits=8, mantissa_bits=7)
    width = 2 * qw + vw
    parts = jnp.stack([hi, mid, lo], axis=1).astype(jnp.bfloat16).reshape(n_ctx, -1)
    extra = -(-parts.shape[-1] // width)
    parts = jnp.pad(parts, ((0, 0), (0, extra * width - parts.shape[-1]))).reshape(n_ctx, extra, width)
    packed = jnp.concatenate(
        [
            jnp.concatenate(
                [
                    queries[0].reshape(seq, n_ctx, qw),
                    keys[0].reshape(seq, n_ctx, qw),
                    values[0].reshape(seq, n_ctx, vw),
                ],
                axis=2,
            ),
            parts.transpose(1, 0, 2),
        ],
        axis=0,
    )
    got = lax.all_to_all(packed, "ctx", 1, 1, tiled=True).transpose(1, 0, 2)
    arrived = got[:, :seq]
    rd = (
        got[:, seq:]
        .reshape(n_ctx, -1)[:, : 3 * 2 * hv_dev * seq]
        .astype(jnp.float32)
        .reshape(n_ctx, 3, 2, hv_dev, seq)
    )
    rd = (rd[:, 0] + rd[:, 1]) + rd[:, 2]
    rates = rd[:, 0].transpose(1, 0, 2)
    gamma = jnp.cumsum(rd[:, 1].transpose(1, 0, 2), axis=-1)
    qc = unit_rows(arrived[..., :qw]) * DK ** (-0.5)
    kc = unit_rows(arrived[..., qw : 2 * qw])
    vc = (
        arrived[..., 2 * qw : 2 * qw + vw]
        .astype(jnp.float32)
        .reshape(n_ctx, seq, hv_dev, DV)
        .transpose(2, 0, 1, 3)
    )

    ordinals = jnp.arange(seq)
    before = ordinals[:, None] > ordinals[None, :]
    upto = ordinals[:, None] >= ordinals[None, :]
    spans = gamma[..., :, None] - gamma[..., None, :]
    pair_decay = jnp.exp(jnp.where(upto, spans, 0.0))
    key_key = jnp.einsum("ntd,nsd->nts", kc, kc, precision=highest)
    lower = jnp.where(before, pair_decay * key_key[None] * rates[..., None, :], 0.0)
    inverse = unit_lower_inverse(lower)
    growth = jnp.exp(gamma)
    right = jnp.concatenate(
        [vc, growth[..., None] * jnp.broadcast_to(kc[None], vc.shape)], axis=-1
    )
    solved = jnp.einsum("hnts,hnsf->hntf", inverse, right, precision=highest)
    solved_values = solved[..., :DV]
    solved_keys = solved[..., DV:]
    tail = rates * jnp.exp(gamma[..., -1:] - gamma)
    weighted = (kc[None] * tail[..., None]).reshape(hv_dev * n_ctx, seq, DK)
    carried = jnp.einsum(
        "btd,btf->bdf", weighted, solved.reshape(hv_dev * n_ctx, seq, DV + DK), precision=highest
    ).reshape(hv_dev, n_ctx, DK, DV + DK)
    growth_last = growth[..., -1]
    key_part = carried[..., DV:]
    offset = carried[..., :DV]
    state = offset[:, 0]
    states = [jnp.zeros_like(state), state]
    for n in range(1, n_ctx - 1):
        state = (
            offset[:, n]
            + growth_last[:, n, None, None] * state
            - jnp.einsum("hde,hef->hdf", key_part[:, n], state, precision=highest)
        )
        states.append(state)
    states = jnp.stack(states, axis=1)
    pseudo = solved_values - jnp.einsum("hntd,hnde->hnte", solved_keys, states, precision=highest)
    query_key = jnp.einsum("ntd,nsd->nts", qc, kc, precision=highest)
    mixing = jnp.where(upto, pair_decay * query_key[None] * rates[..., None, :], 0.0)
    core = growth[..., None] * jnp.einsum("ntd,hnde->hnte", qc, states, precision=highest)
    core = core + jnp.einsum("hnts,hnse->hnte", mixing, pseudo, precision=highest)

    last = accepted[0] - 1
    chunk = last // seq
    local = last % seq
    gamma_chunk = lax.dynamic_index_in_dim(gamma, chunk, axis=1, keepdims=False)
    rates_chunk = lax.dynamic_index_in_dim(rates, chunk, axis=1, keepdims=False)
    pseudo_chunk = lax.dynamic_index_in_dim(pseudo, chunk, axis=1, keepdims=False)
    state_chunk = lax.dynamic_index_in_dim(states, chunk, axis=1, keepdims=False)
    keys_chunk = lax.dynamic_index_in_dim(kc, chunk, axis=0, keepdims=False)
    gamma_at = lax.dynamic_index_in_dim(gamma_chunk, local, axis=1, keepdims=False)
    keep = jnp.where(
        ordinals[None, :] <= local,
        rates_chunk * jnp.exp(jnp.minimum(gamma_at[:, None] - gamma_chunk, 0.0)),
        0.0,
    )
    final_state = jnp.exp(gamma_at)[:, None, None] * state_chunk + jnp.einsum(
        "td,hte->hde", keys_chunk, keep[..., None] * pseudo_chunk, precision=highest
    )
    final_state = final_state[None]

    scale = lax.rsqrt(jnp.mean(core * core, axis=-1, keepdims=True) + 1e-06)
    shaped = (core * scale * norm_gain).astype(jnp.bfloat16)
    shaped = shaped.transpose(1, 2, 0, 3).reshape(n_ctx, seq, vw)
    back = lax.all_to_all(shaped, "ctx", 0, 0, tiled=True)
    gating = jax.nn.silu(gate_input[0].astype(jnp.float32).reshape(seq, n_ctx, vw).transpose(1, 0, 2))
    normed = (back.astype(jnp.float32) * gating).astype(jnp.bfloat16)
    normed = normed.transpose(1, 0, 2).reshape(seq, HV * DV)
    resid = hidden[0].astype(jnp.float32) + jnp.dot(
        normed, w_out, preferred_element_type=jnp.float32
    )
    moe_in = (
        resid * lax.rsqrt(jnp.mean(resid * resid, axis=-1, keepdims=True) + 1e-06) * post_gain
    ).astype(jnp.bfloat16)

    flat_ids = routes[0].reshape(-1)
    onehot = (flat_ids[:, None] == jnp.arange(experts, dtype=jnp.int32)[None, :]).astype(jnp.int32)
    earlier = jnp.cumsum(onehot, axis=0) - onehot
    slot = jnp.sum(earlier * onehot, axis=1)
    target = (flat_ids * cap + slot).reshape(seq, TOPK)
    slots = (
        jnp.arange(experts * cap, dtype=jnp.int32)
        .reshape(n_dev, EXP_DEV, cap)
        .transpose(0, 2, 1)
    )
    hits = target[None, None, None, :, :] == slots[..., None, None]
    dispatch = jnp.sum(jnp.where(hits, 1.0, 0.0), axis=-1).astype(jnp.bfloat16)
    outgoing_rows = jnp.einsum(
        "dcet,tf->dcef", dispatch, moe_in, preferred_element_type=jnp.float32
    ).astype(jnp.bfloat16)
    arrived_rows = lax.all_to_all(
        outgoing_rows, ("ctx", "req"), split_axis=0, concat_axis=0, tiled=True
    )
    both = jnp.einsum(
        "scex,exf->escf", arrived_rows, expert_gate_up, preferred_element_type=jnp.float32
    )
    inner = (jax.nn.silu(both[..., :FFE]) * both[..., FFE:]).astype(jnp.bfloat16)
    result = jnp.einsum(
        "escf,efx->scex", inner, expert_down, preferred_element_type=jnp.float32
    ).astype(jnp.bfloat16)
    returned = lax.all_to_all(result, ("ctx", "req"), split_axis=0, concat_axis=0, tiled=True)
    scores = route_scores[0]
    mix_weights = scores / jnp.sum(scores, axis=-1, keepdims=True)
    combine = jnp.sum(jnp.where(hits, mix_weights, 0.0), axis=-1)
    combine_hi = lax.reduce_precision(combine, exponent_bits=8, mantissa_bits=7)
    combine_lo = combine - combine_hi
    halves = jnp.concatenate([combine_hi, combine_lo], axis=-1).astype(jnp.bfloat16)
    both_out = jnp.einsum(
        "dcet,dcex->tx", halves, returned, preferred_element_type=jnp.float32
    )
    moe_out = both_out[:seq] + both_out[seq:]
    layer_out = (resid + moe_out).astype(jnp.bfloat16)[None]
    return (layer_out, final_state)


def solution(mesh):
    placed = (
        P("req", "ctx", None),
        P("req", "ctx", None),
        P("req", "ctx", None),
        P("req", "ctx", None),
        P("req", None, "ctx"),
        P("req", None, "ctx"),
        P(),
        P(),
        P("req", "ctx", None),
        P(),
        P("req", "ctx", None),
        P("req", "ctx", None),
        P(("ctx", "req"), None, None),
        P(("ctx", "req"), None, None),
        P("req"),
    )
    return jax.shard_map(
        shards,
        mesh=mesh,
        in_specs=placed,
        out_specs=(P("req", "ctx", None), P("req", "ctx", None, None)),
        check_vma=False,
    )
```

```python
import jax
import jax.numpy as jnp
from jax import lax
from jax.sharding import PartitionSpec as P

D = 2048
HK = 8
HV = 16
DK = 128
DV = 128
FFE = 512
TOPK = 10
EXP_DEV = 2


def unit_rows(x):
    x = x.astype(jnp.float32)
    return x * lax.rsqrt(jnp.sum(x * x, axis=-1, keepdims=True) + 1e-06)


def unit_lower_inverse(lower):
    highest = lax.Precision.HIGHEST
    n = lower.shape[-1]
    rows = jnp.arange(n)[:, None]
    cols = jnp.arange(n)[None, :]
    first = (rows // 2 == cols // 2) & (rows % 2 == 1) & (cols % 2 == 0)
    inv = lax.optimization_barrier(jnp.eye(n, dtype=lower.dtype) - jnp.where(first, lower, 0.0))

    def level(i, inv):
        b = jnp.left_shift(jnp.int32(1), i)
        sel = (rows // (2 * b) == cols // (2 * b)) & ((rows // b) % 2 == 1) & ((cols // b) % 2 == 0)
        c = jnp.where(sel, lower, 0.0)
        mc = jnp.einsum("...ij,...jk->...ik", inv, c, precision=highest)
        return inv - jnp.einsum("...ij,...jk->...ik", mc, inv, precision=highest)

    levels = n.bit_length() - 1
    start = 1 + (levels - 1) % 2
    for i in range(1, start):
        inv = level(i, inv)
    inv = lax.fori_loop(
        0, (levels - start) // 2, lambda j, m: level(start + 2 * j + 1, level(start + 2 * j, m)), inv
    )
    return inv


def run_experts(arrived, expert_gate_up, expert_down):
    provider_rows, count, part, width = arrived.shape
    rows = arrived.transpose(1, 0, 2, 3).reshape(count, provider_rows * part, width)
    both = jnp.einsum("erd,edf->erf", rows, expert_gate_up, preferred_element_type=jnp.float32)
    inner = (jax.nn.silu(both[..., :FFE]) * both[..., FFE:]).astype(jnp.bfloat16)
    result = jnp.einsum(
        "erf,efd->erd", inner, expert_down, preferred_element_type=jnp.float32
    ).astype(jnp.bfloat16)
    return result.reshape(count, provider_rows, part, width).transpose(1, 0, 2, 3)


def shards(
    queries,
    keys,
    values,
    gate_input,
    beta,
    log_decay,
    norm_gain,
    w_out,
    hidden,
    post_gain,
    routes,
    route_scores,
    expert_gate_up,
    expert_down,
    accepted,
):
    highest = lax.Precision.HIGHEST
    seq = queries.shape[1]
    n_ctx = lax.axis_size("ctx")
    n_req = lax.axis_size("req")
    n_dev = n_ctx * n_req
    experts = EXP_DEV * n_dev
    cap = max(2, 3 * seq * TOPK // (2 * experts))
    kh_dev = HK // n_ctx
    hv_dev = HV // n_ctx
    qw = kh_dev * DK
    vw = hv_dev * DV

    rates_decay = (
        jnp.stack([beta[0], log_decay[0]]).reshape(2, n_ctx, hv_dev, seq).transpose(1, 0, 2, 3)
    )
    hi = lax.reduce_precision(rates_decay, exponent_bits=8, mantissa_bits=7)
    rest = rates_decay - hi
    mid = lax.reduce_precision(rest, exponent_bits=8, mantissa_bits=7)
    lo = lax.reduce_precision(rest - mid, exponent_bits=8, mantissa_bits=7)
    width = 2 * qw + vw
    parts = jnp.stack([hi, mid, lo], axis=1).astype(jnp.bfloat16).reshape(n_ctx, -1)
    extra = -(-parts.shape[-1] // width)
    parts = jnp.pad(parts, ((0, 0), (0, extra * width - parts.shape[-1]))).reshape(n_ctx, extra, width)
    packed = jnp.concatenate(
        [
            jnp.concatenate(
                [
                    queries[0].reshape(seq, n_ctx, qw),
                    keys[0].reshape(seq, n_ctx, qw),
                    values[0].reshape(seq, n_ctx, vw),
                ],
                axis=2,
            ).transpose(1, 0, 2),
            parts,
        ],
        axis=1,
    )
    got = lax.all_to_all(packed, "ctx", 0, 0, tiled=True)
    arrived = got[:, :seq]
    rd = (
        got[:, seq:]
        .reshape(n_ctx, -1)[:, : 3 * 2 * hv_dev * seq]
        .astype(jnp.float32)
        .reshape(n_ctx, 3, 2, hv_dev, seq)
    )
    rd = (rd[:, 0] + rd[:, 1]) + rd[:, 2]
    rates = rd[:, 0].transpose(1, 0, 2)
    gamma = jnp.cumsum(rd[:, 1].transpose(1, 0, 2), axis=-1)
    qc = unit_rows(arrived[..., :qw]) * DK ** (-0.5)
    kc = unit_rows(arrived[..., qw : 2 * qw])
    vc = (
        arrived[..., 2 * qw : 2 * qw + vw]
        .astype(jnp.float32)
        .reshape(n_ctx, seq, hv_dev, DV)
        .transpose(2, 0, 1, 3)
    )

    ordinals = jnp.arange(seq)
    before = ordinals[:, None] > ordinals[None, :]
    upto = ordinals[:, None] >= ordinals[None, :]
    spans = gamma[..., :, None] - gamma[..., None, :]
    pair_decay = jnp.exp(jnp.where(upto, spans, 0.0))
    key_key = jnp.einsum("ntd,nsd->nts", kc, kc, precision=highest)
    lower = jnp.where(before, pair_decay * key_key[None] * rates[..., None, :], 0.0)
    inverse = unit_lower_inverse(lower)
    growth = jnp.exp(gamma)
    right = jnp.concatenate(
        [vc, growth[..., None] * jnp.broadcast_to(kc[None], vc.shape)], axis=-1
    )
    solved = jnp.einsum("hnts,hnsf->hntf", inverse, right, precision=highest)
    solved_values = solved[..., :DV]
    solved_keys = solved[..., DV:]
    tail = rates * jnp.exp(gamma[..., -1:] - gamma)
    weighted = (kc[None] * tail[..., None]).reshape(hv_dev * n_ctx, seq, DK)
    carried = jnp.einsum(
        "btd,btf->bdf", weighted, solved.reshape(hv_dev * n_ctx, seq, DV + DK), precision=highest
    ).reshape(hv_dev, n_ctx, DK, DV + DK)
    growth_last = growth[..., -1]
    key_part = carried[..., DV:]
    offset = carried[..., :DV]
    state = offset[:, 0]
    states = [jnp.zeros_like(state), state]
    for n in range(1, n_ctx - 1):
        state = (
            offset[:, n]
            + growth_last[:, n, None, None] * state
            - jnp.einsum("hde,hef->hdf", key_part[:, n], state, precision=highest)
        )
        states.append(state)
    states = jnp.stack(states, axis=1)
    pseudo = solved_values - jnp.einsum("hntd,hnde->hnte", solved_keys, states, precision=highest)
    query_key = jnp.einsum("ntd,nsd->nts", qc, kc, precision=highest)
    mixing = jnp.where(upto, pair_decay * query_key[None] * rates[..., None, :], 0.0)
    core = growth[..., None] * jnp.einsum("ntd,hnde->hnte", qc, states, precision=highest)
    core = core + jnp.einsum("hnts,hnse->hnte", mixing, pseudo, precision=highest)

    last = accepted[0] - 1
    chunk = last // seq
    local = last % seq
    gamma_chunk = lax.dynamic_index_in_dim(gamma, chunk, axis=1, keepdims=False)
    rates_chunk = lax.dynamic_index_in_dim(rates, chunk, axis=1, keepdims=False)
    pseudo_chunk = lax.dynamic_index_in_dim(pseudo, chunk, axis=1, keepdims=False)
    state_chunk = lax.dynamic_index_in_dim(states, chunk, axis=1, keepdims=False)
    keys_chunk = lax.dynamic_index_in_dim(kc, chunk, axis=0, keepdims=False)
    gamma_at = lax.dynamic_index_in_dim(gamma_chunk, local, axis=1, keepdims=False)
    keep = jnp.where(
        ordinals[None, :] <= local,
        rates_chunk * jnp.exp(jnp.minimum(gamma_at[:, None] - gamma_chunk, 0.0)),
        0.0,
    )
    final_state = jnp.exp(gamma_at)[:, None, None] * state_chunk + jnp.einsum(
        "td,hte->hde", keys_chunk, keep[..., None] * pseudo_chunk, precision=highest
    )
    final_state = final_state[None]

    scale = lax.rsqrt(jnp.mean(core * core, axis=-1, keepdims=True) + 1e-06)
    shaped = (core * scale * norm_gain).astype(jnp.bfloat16)
    shaped = shaped.transpose(1, 2, 0, 3).reshape(n_ctx, seq, vw)
    back = lax.all_to_all(shaped, "ctx", 0, 0, tiled=True)
    gating = jax.nn.silu(gate_input[0].astype(jnp.float32).reshape(seq, n_ctx, vw).transpose(1, 0, 2))
    normed = (back.astype(jnp.float32) * gating).astype(jnp.bfloat16)
    resid = hidden[0].astype(jnp.float32) + jnp.einsum(
        "jtf,jfd->td",
        normed,
        w_out.reshape(n_ctx, vw, D),
        preferred_element_type=jnp.float32,
    )
    moe_in = (
        resid * lax.rsqrt(jnp.mean(resid * resid, axis=-1, keepdims=True) + 1e-06) * post_gain
    ).astype(jnp.bfloat16)

    flat_ids = routes[0].reshape(-1)
    onehot = (flat_ids[:, None] == jnp.arange(experts, dtype=jnp.int32)[None, :]).astype(jnp.int32)
    earlier = jnp.cumsum(onehot, axis=0) - onehot
    slot = jnp.sum(earlier * onehot, axis=1)
    target = (flat_ids * cap + slot).reshape(seq, TOPK)
    slots = (
        jnp.arange(experts * cap, dtype=jnp.int32)
        .reshape(n_dev, EXP_DEV, cap)
        .transpose(0, 2, 1)
    )
    hits = target[None, None, None, :, :] == slots[..., None, None]
    dispatch = jnp.sum(jnp.where(hits, 1.0, 0.0), axis=-1).astype(jnp.bfloat16)
    outgoing_rows = jnp.einsum(
        "dcet,tf->dcef", dispatch, moe_in, preferred_element_type=jnp.float32
    ).astype(jnp.bfloat16)
    arrived_rows = lax.all_to_all(
        outgoing_rows, ("ctx", "req"), split_axis=0, concat_axis=0, tiled=True
    )
    both = jnp.einsum(
        "scex,exf->escf", arrived_rows, expert_gate_up, preferred_element_type=jnp.float32
    )
    inner = (jax.nn.silu(both[..., :FFE]) * both[..., FFE:]).astype(jnp.bfloat16)
    result = jnp.einsum(
        "escf,efx->scex", inner, expert_down, preferred_element_type=jnp.float32
    ).astype(jnp.bfloat16)
    returned = lax.all_to_all(result, ("ctx", "req"), split_axis=0, concat_axis=0, tiled=True)
    scores = route_scores[0]
    mix_weights = scores / jnp.sum(scores, axis=-1, keepdims=True)
    combine = jnp.sum(jnp.where(hits, mix_weights, 0.0), axis=-1)
    combine_hi = lax.reduce_precision(combine, exponent_bits=8, mantissa_bits=7)
    combine_lo = combine - combine_hi
    halves = jnp.concatenate([combine_hi, combine_lo], axis=-1).astype(jnp.bfloat16)
    both_out = jnp.einsum(
        "dcet,dcex->tx", halves, returned, preferred_element_type=jnp.float32
    )
    moe_out = both_out[:seq] + both_out[seq:]
    layer_out = (resid + moe_out).astype(jnp.bfloat16)[None]
    return (layer_out, final_state)


def solution(mesh):
    placed = (
        P("req", "ctx", None),
        P("req", "ctx", None),
        P("req", "ctx", None),
        P("req", "ctx", None),
        P("req", None, "ctx"),
        P("req", None, "ctx"),
        P(),
        P(),
        P("req", "ctx", None),
        P(),
        P("req", "ctx", None),
        P("req", "ctx", None),
        P(("ctx", "req"), None, None),
        P(("ctx", "req"), None, None),
        P("req"),
    )
    return jax.shard_map(
        shards,
        mesh=mesh,
        in_specs=placed,
        out_specs=(P("req", "ctx", None), P("req", "ctx", None, None)),
        check_vma=False,
    )
```

```python
import jax
import jax.numpy as jnp
from jax import lax
from jax.sharding import PartitionSpec as P

D = 2048
HK = 8
HV = 16
DK = 128
DV = 128
FFE = 512
TOPK = 10
EXP_DEV = 2


def unit_rows(x):
    x = x.astype(jnp.float32)
    return x * lax.rsqrt(jnp.sum(x * x, axis=-1, keepdims=True) + 1e-06)


def unit_lower_inverse(lower):
    highest = lax.Precision.HIGHEST
    n = lower.shape[-1]
    rows = jnp.arange(n)[:, None]
    cols = jnp.arange(n)[None, :]
    first = (rows // 2 == cols // 2) & (rows % 2 == 1) & (cols % 2 == 0)
    inv = lax.optimization_barrier(jnp.eye(n, dtype=lower.dtype) - jnp.where(first, lower, 0.0))

    def level(i, inv):
        b = jnp.left_shift(jnp.int32(1), i)
        sel = (rows // (2 * b) == cols // (2 * b)) & ((rows // b) % 2 == 1) & ((cols // b) % 2 == 0)
        c = jnp.where(sel, lower, 0.0)
        mc = jnp.einsum("...ij,...jk->...ik", inv, c, precision=highest)
        return inv - jnp.einsum("...ij,...jk->...ik", mc, inv, precision=highest)

    levels = n.bit_length() - 1
    start = 1 + (levels - 1) % 2
    for i in range(1, start):
        inv = level(i, inv)
    inv = lax.fori_loop(
        0, (levels - start) // 2, lambda j, m: level(start + 2 * j + 1, level(start + 2 * j, m)), inv
    )
    return inv


def run_experts(arrived, expert_gate_up, expert_down):
    provider_rows, count, part, width = arrived.shape
    rows = arrived.transpose(1, 0, 2, 3).reshape(count, provider_rows * part, width)
    both = jnp.einsum("erd,edf->erf", rows, expert_gate_up, preferred_element_type=jnp.float32)
    inner = (jax.nn.silu(both[..., :FFE]) * both[..., FFE:]).astype(jnp.bfloat16)
    result = jnp.einsum(
        "erf,efd->erd", inner, expert_down, preferred_element_type=jnp.float32
    ).astype(jnp.bfloat16)
    return result.reshape(count, provider_rows, part, width).transpose(1, 0, 2, 3)


def shards(
    queries,
    keys,
    values,
    gate_input,
    beta,
    log_decay,
    norm_gain,
    w_out,
    hidden,
    post_gain,
    routes,
    route_scores,
    expert_gate_up,
    expert_down,
    accepted,
):
    highest = lax.Precision.HIGHEST
    seq = queries.shape[1]
    n_ctx = lax.axis_size("ctx")
    n_req = lax.axis_size("req")
    n_dev = n_ctx * n_req
    experts = EXP_DEV * n_dev
    cap = max(2, 3 * seq * TOPK // (2 * experts))
    kh_dev = HK // n_ctx
    hv_dev = HV // n_ctx
    qw = kh_dev * DK
    vw = hv_dev * DV

    rates_decay = (
        jnp.stack([beta[0], log_decay[0]]).reshape(2, n_ctx, hv_dev, seq).transpose(1, 0, 2, 3)
    )
    hi = lax.reduce_precision(rates_decay, exponent_bits=8, mantissa_bits=7)
    rest = rates_decay - hi
    mid = lax.reduce_precision(rest, exponent_bits=8, mantissa_bits=7)
    lo = lax.reduce_precision(rest - mid, exponent_bits=8, mantissa_bits=7)
    width = 2 * qw + vw
    parts = jnp.stack([hi, mid, lo], axis=1).astype(jnp.bfloat16).reshape(n_ctx, -1)
    extra = -(-parts.shape[-1] // width)
    parts = jnp.pad(parts, ((0, 0), (0, extra * width - parts.shape[-1]))).reshape(n_ctx, extra, width)
    packed = jnp.concatenate(
        [
            jnp.concatenate(
                [
                    queries[0].reshape(seq, n_ctx, qw),
                    keys[0].reshape(seq, n_ctx, qw),
                    values[0].reshape(seq, n_ctx, vw),
                ],
                axis=2,
            ).transpose(1, 0, 2),
            parts,
        ],
        axis=1,
    )
    flat_ids = routes[0].reshape(-1)
    onehot = (flat_ids[:, None] == jnp.arange(experts, dtype=jnp.int32)[None, :]).astype(jnp.int32)
    earlier = jnp.cumsum(onehot, axis=0) - onehot
    slot = jnp.sum(earlier * onehot, axis=1)
    target = (flat_ids * cap + slot).reshape(seq, TOPK)
    slots = (
        jnp.arange(experts * cap, dtype=jnp.int32)
        .reshape(n_dev, EXP_DEV, cap)
        .transpose(0, 2, 1)
    )
    hits = target[None, None, None, :, :] == slots[..., None, None]
    dispatch = jnp.sum(jnp.where(hits, 1.0, 0.0), axis=-1).astype(jnp.bfloat16)
    scores = route_scores[0]
    mix_weights = scores / jnp.sum(scores, axis=-1, keepdims=True)
    combine = jnp.sum(jnp.where(hits, mix_weights, 0.0), axis=-1)
    got = lax.all_to_all(packed, "ctx", 0, 0, tiled=True)
    got, dispatch, combine = lax.optimization_barrier((got, dispatch, combine))
    arrived = got[:, :seq]
    rd = (
        got[:, seq:]
        .reshape(n_ctx, -1)[:, : 3 * 2 * hv_dev * seq]
        .astype(jnp.float32)
        .reshape(n_ctx, 3, 2, hv_dev, seq)
    )
    rd = (rd[:, 0] + rd[:, 1]) + rd[:, 2]
    rates = rd[:, 0].transpose(1, 0, 2)
    gamma = jnp.cumsum(rd[:, 1].transpose(1, 0, 2), axis=-1)
    qc = unit_rows(arrived[..., :qw]) * DK ** (-0.5)
    kc = unit_rows(arrived[..., qw : 2 * qw])
    vc = (
        arrived[..., 2 * qw : 2 * qw + vw]
        .astype(jnp.float32)
        .reshape(n_ctx, seq, hv_dev, DV)
        .transpose(2, 0, 1, 3)
    )

    ordinals = jnp.arange(seq)
    before = ordinals[:, None] > ordinals[None, :]
    upto = ordinals[:, None] >= ordinals[None, :]
    spans = gamma[..., :, None] - gamma[..., None, :]
    pair_decay = jnp.exp(jnp.where(upto, spans, 0.0))
    key_key = jnp.einsum("ntd,nsd->nts", kc, kc, precision=highest)
    lower = jnp.where(before, pair_decay * key_key[None] * rates[..., None, :], 0.0)
    inverse = unit_lower_inverse(lower)
    growth = jnp.exp(gamma)
    right = jnp.concatenate(
        [vc, growth[..., None] * jnp.broadcast_to(kc[None], vc.shape)], axis=-1
    )
    solved = jnp.einsum("hnts,hnsf->hntf", inverse, right, precision=highest)
    solved_values = solved[..., :DV]
    solved_keys = solved[..., DV:]
    tail = rates * jnp.exp(gamma[..., -1:] - gamma)
    weighted = (kc[None] * tail[..., None]).reshape(hv_dev * n_ctx, seq, DK)
    carried = jnp.einsum(
        "btd,btf->bdf", weighted, solved.reshape(hv_dev * n_ctx, seq, DV + DK), precision=highest
    ).reshape(hv_dev, n_ctx, DK, DV + DK)
    growth_last = growth[..., -1]
    key_part = carried[..., DV:]
    offset = carried[..., :DV]
    state = offset[:, 0]
    states = [jnp.zeros_like(state), state]
    for n in range(1, n_ctx - 1):
        state = (
            offset[:, n]
            + growth_last[:, n, None, None] * state
            - jnp.einsum("hde,hef->hdf", key_part[:, n], state, precision=highest)
        )
        states.append(state)
    states = jnp.stack(states, axis=1)
    pseudo = solved_values - jnp.einsum("hntd,hnde->hnte", solved_keys, states, precision=highest)
    query_key = jnp.einsum("ntd,nsd->nts", qc, kc, precision=highest)
    mixing = jnp.where(upto, pair_decay * query_key[None] * rates[..., None, :], 0.0)
    core = growth[..., None] * jnp.einsum("ntd,hnde->hnte", qc, states, precision=highest)
    core = core + jnp.einsum("hnts,hnse->hnte", mixing, pseudo, precision=highest)

    last = accepted[0] - 1
    chunk = last // seq
    local = last % seq
    gamma_chunk = lax.dynamic_index_in_dim(gamma, chunk, axis=1, keepdims=False)
    rates_chunk = lax.dynamic_index_in_dim(rates, chunk, axis=1, keepdims=False)
    pseudo_chunk = lax.dynamic_index_in_dim(pseudo, chunk, axis=1, keepdims=False)
    state_chunk = lax.dynamic_index_in_dim(states, chunk, axis=1, keepdims=False)
    keys_chunk = lax.dynamic_index_in_dim(kc, chunk, axis=0, keepdims=False)
    gamma_at = lax.dynamic_index_in_dim(gamma_chunk, local, axis=1, keepdims=False)
    keep = jnp.where(
        ordinals[None, :] <= local,
        rates_chunk * jnp.exp(jnp.minimum(gamma_at[:, None] - gamma_chunk, 0.0)),
        0.0,
    )
    final_state = jnp.exp(gamma_at)[:, None, None] * state_chunk + jnp.einsum(
        "td,hte->hde", keys_chunk, keep[..., None] * pseudo_chunk, precision=highest
    )
    final_state = final_state[None]

    scale = lax.rsqrt(jnp.mean(core * core, axis=-1, keepdims=True) + 1e-06)
    shaped = (core * scale * norm_gain).astype(jnp.bfloat16)
    shaped = shaped.transpose(1, 2, 0, 3).reshape(n_ctx, seq, vw)
    back = lax.all_to_all(shaped, "ctx", 0, 0, tiled=True)
    gating = jax.nn.silu(gate_input[0].astype(jnp.float32).reshape(seq, n_ctx, vw).transpose(1, 0, 2))
    normed = (back.astype(jnp.float32) * gating).astype(jnp.bfloat16)
    resid = hidden[0].astype(jnp.float32) + jnp.einsum(
        "jtf,jfd->td",
        normed,
        w_out.reshape(n_ctx, vw, D),
        preferred_element_type=jnp.float32,
    )
    moe_in = (
        resid * lax.rsqrt(jnp.mean(resid * resid, axis=-1, keepdims=True) + 1e-06) * post_gain
    ).astype(jnp.bfloat16)

    outgoing_rows = jnp.einsum(
        "dcet,tf->dcef", dispatch, moe_in, preferred_element_type=jnp.float32
    ).astype(jnp.bfloat16)
    arrived_rows = lax.all_to_all(
        outgoing_rows, ("ctx", "req"), split_axis=0, concat_axis=0, tiled=True
    )
    both = jnp.einsum(
        "scex,exf->escf", arrived_rows, expert_gate_up, preferred_element_type=jnp.float32
    )
    inner = (jax.nn.silu(both[..., :FFE]) * both[..., FFE:]).astype(jnp.bfloat16)
    result = jnp.einsum(
        "escf,efx->scex", inner, expert_down, preferred_element_type=jnp.float32
    ).astype(jnp.bfloat16)
    returned = lax.all_to_all(result, ("ctx", "req"), split_axis=0, concat_axis=0, tiled=True)
    combine_hi = lax.reduce_precision(combine, exponent_bits=8, mantissa_bits=7)
    combine_lo = combine - combine_hi
    halves = jnp.concatenate([combine_hi, combine_lo], axis=-1).astype(jnp.bfloat16)
    both_out = jnp.einsum(
        "dcet,dcex->tx", halves, returned, preferred_element_type=jnp.float32
    )
    moe_out = both_out[:seq] + both_out[seq:]
    layer_out = (resid + moe_out).astype(jnp.bfloat16)[None]
    return (layer_out, final_state)


def solution(mesh):
    placed = (
        P("req", "ctx", None),
        P("req", "ctx", None),
        P("req", "ctx", None),
        P("req", "ctx", None),
        P("req", None, "ctx"),
        P("req", None, "ctx"),
        P(),
        P(),
        P("req", "ctx", None),
        P(),
        P("req", "ctx", None),
        P("req", "ctx", None),
        P(("ctx", "req"), None, None),
        P(("ctx", "req"), None, None),
        P("req"),
    )
    return jax.shard_map(
        shards,
        mesh=mesh,
        in_specs=placed,
        out_specs=(P("req", "ctx", None), P("req", "ctx", None, None)),
        check_vma=False,
    )
```
